128 devices in a mesh: slab: 32 (over y, x, core), grp: 4 (over z).
Axes of the slice: x: 4, y: 4, z: 4, core: 2. Of those that a mesh axis runs over, the one named last changes fastest.
Arguments:
- images: float32 [128, 512, 512], P(('slab', 'grp')), may hold values from -6 to 6
- crossing_row: int32 [128, 1024], P(('slab', 'grp')), may hold values from 0 to 511
- crossing_dest: int32 [128, 1024, 1], P(('slab', 'grp')), may hold values from 0 to 127; in each aligned block of 1024 rows (0 to 1023, 1024 to 2047, ..., all dimensions but the last counted through in order) at most 16 rows name the same one
- crossing_line: int32 [128, 1024], P(('slab', 'grp')), may hold values from 0 to 127
- interp_weight: bfloat16 [128, 1024, 16], P(('slab', 'grp')), may hold values from 0 to 1
Outputs:
- reconstruction: float32 [2, 512, 512, 512], P(None, 'slab', 'grp')
The draws below stay inside these ranges and needn't reach their ends.
Inputs may be any that keep to these rules, and one draw needn't show every extreme that they name: `crossing_dest`: within the rows of one device (1024 crossings), at most 16 crossings name the same destination, and in every draw some destination is named by exactly 16 of them.
All inputs are finite; a program needn't handle non-finite values.
Results may differ from the reference program's by a relative error of at most 0.0029.
Values may be sent and summed in bfloat16 or wider, within the bound.
No kernel may reach another device: no remote copies, remote signals or barrier semaphores. Data moves between devices by JAX's collectives and lax.ppermute only.
A program may use at most 128 MiB of HBM per device.

```python
import math
import jax
import jax.numpy as jnp
import numpy as np
from jax import lax

L = 512
P_DEV = 1
K = 1024
GROUPS = 4
PARTICLES = 128
ZP = 16
YQ = 128
CAP = 16
N_SLAB = 32
N_GRP = 4


def place_ends(array, key, least, top_value):
    index_at = [jax.random.randint(jax.random.fold_in(key, axis), (), 0, length) for axis, length in enumerate(array.shape)]
    longest = array.shape.index(max(array.shape))
    next_to = index_at[:longest] + [(index_at[longest] + 1) % array.shape[longest]] + index_at[longest + 1:]
    return array.at[tuple(index_at)].set(least).at[tuple(next_to)].set(top_value)


def levels(own_key, shape, shards, low, high):
    loudness, own = 1.0, jax.random.fold_in(own_key, 6)
    for axis_at, blocks in shards:
        heights = jnp.exp(jax.random.uniform(jax.random.fold_in(own, axis_at), (blocks,), jnp.float32, low / len(shards), high / len(shards)))
        loudness = loudness * jnp.repeat(heights, shape[axis_at] // blocks).reshape([-1 if axis == axis_at else 1 for axis in range(len(shape))])
    return loudness


def routed_block(stream_key, own, number, rows, number_of, top, reach, skew):
    order = jax.random.permutation(stream_key, number_of)
    packed, ordinary = portions_of(number_of, rows * top, reach, skew, True), portions_of(number_of, rows * top, reach, skew, False)
    places = jnp.arange(number_of)

    def named(tallies, rotation):
        used = int((tallies > 0).sum())
        fixed = max(1, used // 4)
        moved = fixed + (places - fixed + rotation * (used - fixed)) % max(1, number_of - fixed)
        return jnp.zeros((number_of,), jnp.int32).at[order[jnp.where(places < fixed, places, moved)]].set(jnp.asarray(tallies, jnp.int32))

    tallies = jnp.where(number % 4 == 0, named(packed, number // 4), named(ordinary, number - number // 4 - 1))
    mixed = jax.random.permutation(jax.random.fold_in(own, 3), number_of)
    source_of, receiver = mixed[0:number_of // 2 * 2:2], mixed[1:number_of // 2 * 2:2]
    margin = jnp.minimum(tallies[source_of] - 1, reach - tallies[receiver]) // 2
    margin = jnp.where((source_of == order[0]) | (receiver == order[0]) | (tallies[receiver] == 0), 0, jnp.maximum(margin, 0))
    moved = jax.random.randint(jax.random.fold_in(own, 4), (number_of // 2,), 0, 1 << 20) % (margin + 1)
    tallies = tallies.at[source_of].add(-moved).at[receiver].add(moved)
    members = jnp.searchsorted(jnp.cumsum(tallies), jnp.arange(rows * top), side="right").astype(jnp.int32)
    table = members.reshape(top, rows).T
    table = table[jax.random.permutation(jax.random.fold_in(own, 1), rows)]
    rotation = jax.random.randint(jax.random.fold_in(own, 2), (rows, 1), 0, top)
    return jnp.take_along_axis(table, (jnp.arange(top)[None, :] + rotation) % top, axis=1)


def portions_of(number_of, total, reach, slope, full):
    weights = [(1 << 20) // math.isqrt(standing ** slope) + 1 for standing in range(1, number_of + 1)]
    largest = reach if full else min(reach, max(-(-total // number_of), total * weights[0] // sum(weights)))
    least = 1 if total - largest >= number_of - 1 else 0
    holding, spare = [largest] + [least] * (number_of - 1), total - largest - least * (number_of - 1)
    while spare > 0:
        movable = [i for i in range(1, number_of) if holding[i] < largest] or [i for i in range(1, number_of) if holding[i] < reach]
        mass, remaining = sum([weights[i] for i in movable]), spare
        for i in movable:
            addition = min(reach - holding[i], max(1, remaining * weights[i] // mass), spare)
            holding[i] = holding[i] + addition
            spare = spare - addition
    return np.array(holding)


def normal_values(own_key, dims, scale, most, split=(), kind=jnp.bfloat16):
    loudness = levels(own_key, dims, split, -0.22, 0.18) if split else 1.0
    drawn = jax.random.normal(own_key, dims, jnp.float32) * scale * loudness
    return jnp.minimum(jnp.maximum(drawn, -most), most).astype(kind)


def setup_inputs(seed: int = 0) -> dict:
    key_list = jax.random.split(jax.random.key(seed), 6)
    images = normal_values(key_list[0], (PARTICLES, L, L), 1.0, 6.0, ((0, 128),), jnp.float32)
    crossing_row = place_ends(jax.random.randint(key_list[1], (PARTICLES, K), 0, L), jax.random.fold_in(key_list[1], 1), 0, L - 1).astype(jnp.int32)
    crossing_dest_keys = jax.random.split(jax.random.fold_in(key_list[2], 1), PARTICLES * K // (P_DEV * K))
    crossing_dest_turns = jax.random.permutation(jax.random.fold_in(key_list[2], 3), PARTICLES * K // (P_DEV * K))
    crossing_dest = jax.vmap(lambda own, number: routed_block(jax.random.fold_in(key_list[2], 2), own, number, P_DEV * K, N_SLAB * N_GRP, 1, CAP, 2))(crossing_dest_keys, crossing_dest_turns).reshape((PARTICLES, K, 1))
    crossing_line = place_ends(jax.random.randint(key_list[3], (PARTICLES, K), 0, YQ), jax.random.fold_in(key_list[3], 1), 0, YQ - 1).astype(jnp.int32)
    interp_weight = jnp.clip(1.0 * jax.random.uniform(key_list[4], (PARTICLES, K, ZP), jnp.float32) ** levels(key_list[4], (PARTICLES, K, ZP), ((0, 128),), -0.2, 0.2), 0.0, 1.0).astype(jnp.bfloat16)
    return dict(images=images, crossing_row=crossing_row, crossing_dest=crossing_dest, crossing_line=crossing_line, interp_weight=interp_weight)


def reference(images, crossing_row, crossing_dest, crossing_line, interp_weight):
    plane_grid = jnp.arange(ZP, dtype=jnp.int32)

    def add_particle(volume, pieces):
        one_image, rows_of, dest_of, line_of, weight_of = pieces
        spectrum = jnp.fft.fft2(one_image, norm="ortho")
        picked = spectrum[rows_of]
        rows_low = jnp.concatenate([jnp.real(picked), jnp.imag(picked)], axis=1).astype(jnp.bfloat16)
        target = dest_of[:, 0]
        slab_of = target // GROUPS
        line_index = ((target % GROUPS) * YQ + line_of).astype(jnp.int32)
        plane_index = (slab_of[:, None] * ZP + plane_grid[None, :]).astype(jnp.int32)
        line_all = jnp.broadcast_to(line_index[:, None], plane_index.shape)
        spread_terms = weight_of.astype(jnp.float32)[:, :, None] * rows_low.astype(jnp.float32)[:, None, :]
        return volume.at[plane_index, line_all].add(spread_terms), None

    empty_volume = jnp.zeros((L, L, 2 * L), jnp.float32)
    volume, _ = lax.scan(add_particle, empty_volume, (images, crossing_row, crossing_dest, crossing_line, interp_weight))
    spectrum_field = lax.complex(volume[:, :, :L], volume[:, :, L:])
    spectrum_field = jnp.fft.ifft(spectrum_field, axis=2, norm="ortho")
    spectrum_field = jnp.fft.ifft(spectrum_field, axis=0, norm="ortho")
    stacked = jnp.stack([jnp.real(spectrum_field), jnp.imag(spectrum_field)])
    return jnp.transpose(stacked, (0, 3, 2, 1)).astype(jnp.float32)
```

```python
import math

import jax
import jax.numpy as jnp
import ml_dtypes
import numpy as np
from jax import lax
from jax.sharding import PartitionSpec as P


def twiddles(length):
    index_grid = np.arange(length)
    phase_angle = (np.outer(index_grid, index_grid) % length) * (2.0 * np.pi / length)
    norm_scale = 1.0 / math.sqrt(length)
    return (np.cos(phase_angle) * norm_scale, np.sin(phase_angle) * norm_scale)


def halves(values):
    high = values.astype(ml_dtypes.bfloat16)
    low = (values - high.astype(np.float64)).astype(ml_dtypes.bfloat16)
    return jnp.asarray(high), jnp.asarray(low)


def local(images, crossing_row, crossing_dest, crossing_line, interp_weight):
    high = lax.Precision.HIGH
    length = images.shape[1]
    crossings = crossing_row.shape[1]
    slab_count = lax.axis_size("slab")
    group_count = lax.axis_size("grp")
    devices_all = slab_count * group_count
    planes = length // slab_count
    lines_per = length // group_count
    capacity = 2 * crossings // devices_all
    slot_count = devices_all * capacity
    x_block = length // slab_count
    cosine_table, sine_table = twiddles(length)

    image = images[0]
    forward_y = jnp.asarray(np.concatenate([cosine_table, -sine_table], axis=0), jnp.float32)
    along_y = jnp.dot(forward_y, image, precision=high, preferred_element_type=jnp.float32)
    from_real = jnp.asarray(np.concatenate([cosine_table, -sine_table], axis=1), jnp.float32)
    from_imag = jnp.asarray(np.concatenate([sine_table, cosine_table], axis=1), jnp.float32)
    spectra = jnp.dot(along_y[:length], from_real, precision=high, preferred_element_type=jnp.float32)
    spectra = spectra + jnp.dot(along_y[length:], from_imag, precision=high, preferred_element_type=jnp.float32)
    spectra_low = spectra.astype(jnp.bfloat16)

    row_hits = (crossing_row[0][:, None] == jnp.arange(length, dtype=jnp.int32)[None, :]).astype(
        jnp.bfloat16
    )
    slice_rows = jnp.dot(row_hits, spectra_low, preferred_element_type=jnp.float32).astype(jnp.bfloat16)
    extra = 128
    meta_grid = jnp.arange(extra, dtype=jnp.int32)[None, :]
    weight_place = jnp.asarray(np.eye(planes, extra), jnp.bfloat16)
    meta = jnp.dot(interp_weight[0], weight_place, preferred_element_type=jnp.float32)
    meta = meta + jnp.where(meta_grid == planes, crossing_line[0][:, None].astype(jnp.float32), 0.0)
    payload = jnp.concatenate([slice_rows, meta.astype(jnp.bfloat16)], axis=1)

    destination = crossing_dest[0, :, 0]
    onehot = (destination[:, None] == jnp.arange(devices_all, dtype=jnp.int32)[None, :]).astype(jnp.int32)
    earlier = jnp.cumsum(onehot, axis=0) - onehot
    slot_within = jnp.sum(earlier * onehot, axis=1)
    position = destination * capacity + slot_within
    placing = (jnp.arange(slot_count, dtype=jnp.int32)[:, None] == position[None, :]).astype(jnp.bfloat16)
    send = jnp.dot(placing, payload, preferred_element_type=jnp.float32).astype(jnp.bfloat16)
    width = 2 * length + extra
    got = lax.all_to_all(
        send.reshape(devices_all, capacity, width), ("slab", "grp"), split_axis=0, concat_axis=0, tiled=True
    ).reshape(slot_count, width)

    rows_in = got[:, : 2 * length]
    weight_in = got[:, 2 * length : 2 * length + planes]
    line_in = got[:, 2 * length + planes].astype(jnp.float32)
    line_grid = jnp.arange(lines_per, dtype=jnp.float32)[None, None, :]
    spread = jnp.where(line_in[:, None, None] == line_grid, weight_in[:, :, None], jnp.zeros((), jnp.bfloat16))
    spread = spread.reshape(slot_count, planes * lines_per)
    volume = lax.dot_general(
        rows_in, spread, (((0,), (0,)), ((), ())), preferred_element_type=jnp.float32
    )

    inverse = np.concatenate(
        [
            np.concatenate([cosine_table, sine_table], axis=1),
            np.concatenate([-sine_table, cosine_table], axis=1),
        ],
        axis=0,
    )
    inverse_blocked = jnp.asarray(
        inverse.reshape(2 * length, 2, slab_count, x_block).transpose(0, 2, 1, 3).reshape(2 * length, 2 * length),
        jnp.float32,
    )
    along_x = lax.dot_general(
        inverse_blocked, volume, (((0,), (0,)), ((), ())), precision=high, preferred_element_type=jnp.float32
    )
    along_x = along_x.astype(jnp.bfloat16).reshape(slab_count, 2, x_block, planes, lines_per)
    pencil = lax.all_to_all(along_x, "slab", split_axis=0, concat_axis=0, tiled=True)

    lhs = pencil.transpose(2, 4, 0, 1, 3).reshape(x_block * lines_per, 2 * length)
    z_table = inverse.reshape(2, slab_count, planes, 2 * length).transpose(1, 0, 2, 3).reshape(2 * length, 2 * length)
    z_high, z_low = halves(z_table)
    parts = []
    for part in range(2):
        columns = slice(part * length, (part + 1) * length)
        flat = jnp.dot(lhs, z_high[:, columns], preferred_element_type=jnp.float32)
        flat = flat + jnp.dot(lhs, z_low[:, columns], preferred_element_type=jnp.float32)
        parts.append(flat.reshape(x_block, lines_per, length))
    result = jnp.stack(parts)
    return result


def solution(mesh):
    return jax.shard_map(
        local,
        mesh=mesh,
        in_specs=(
            P(("slab", "grp"), None, None),
            P(("slab", "grp"), None),
            P(("slab", "grp"), None, None),
            P(("slab", "grp"), None),
            P(("slab", "grp"), None, None),
        ),
        out_specs=P(None, "slab", "grp", None),
        check_vma=False,
    )
```

```python
import math

import jax
import jax.numpy as jnp
import ml_dtypes
import numpy as np
from jax import lax
from jax.sharding import PartitionSpec as P


def twiddles(length):
    index_grid = np.arange(length)
    phase_angle = (np.outer(index_grid, index_grid) % length) * (2.0 * np.pi / length)
    norm_scale = 1.0 / math.sqrt(length)
    return (np.cos(phase_angle) * norm_scale, np.sin(phase_angle) * norm_scale)


def halves(values):
    high = values.astype(ml_dtypes.bfloat16)
    low = (values - high.astype(np.float64)).astype(ml_dtypes.bfloat16)
    return jnp.asarray(high), jnp.asarray(low)


def local(images, crossing_row, crossing_dest, crossing_line, interp_weight):
    high = lax.Precision.HIGH
    length = images.shape[1]
    crossings = crossing_row.shape[1]
    slab_count = lax.axis_size("slab")
    group_count = lax.axis_size("grp")
    devices_all = slab_count * group_count
    planes = length // slab_count
    lines_per = length // group_count
    capacity = 2 * crossings // devices_all
    slot_count = devices_all * capacity
    x_block = length // slab_count
    cosine_table, sine_table = twiddles(length)

    image = images[0]
    forward_y = jnp.asarray(np.concatenate([cosine_table, -sine_table], axis=0), jnp.float32)
    along_y = jnp.dot(forward_y, image, precision=high, preferred_element_type=jnp.float32)
    from_real = jnp.asarray(np.concatenate([cosine_table, -sine_table], axis=1), jnp.float32)
    from_imag = jnp.asarray(np.concatenate([sine_table, cosine_table], axis=1), jnp.float32)
    spectra = jnp.dot(along_y[:length], from_real, precision=high, preferred_element_type=jnp.float32)
    spectra = spectra + jnp.dot(along_y[length:], from_imag, precision=high, preferred_element_type=jnp.float32)
    spectra_low = spectra.astype(jnp.bfloat16)

    row_hits = (crossing_row[0][:, None] == jnp.arange(length, dtype=jnp.int32)[None, :]).astype(
        jnp.bfloat16
    )
    slice_rows = jnp.dot(row_hits, spectra_low, preferred_element_type=jnp.float32).astype(jnp.bfloat16)
    extra = 128
    meta_grid = jnp.arange(extra, dtype=jnp.int32)[None, :]
    weight_place = jnp.asarray(np.eye(planes, extra), jnp.bfloat16)
    meta = jnp.dot(interp_weight[0], weight_place, preferred_element_type=jnp.float32)
    meta = meta + jnp.where(meta_grid == planes, crossing_line[0][:, None].astype(jnp.float32), 0.0)
    payload = jnp.concatenate([slice_rows, meta.astype(jnp.bfloat16)], axis=1)

    destination = crossing_dest[0, :, 0]
    onehot = (destination[:, None] == jnp.arange(devices_all, dtype=jnp.int32)[None, :]).astype(jnp.int32)
    earlier = jnp.cumsum(onehot, axis=0) - onehot
    slot_within = jnp.sum(earlier * onehot, axis=1)
    position = destination * capacity + slot_within
    placing = (jnp.arange(slot_count, dtype=jnp.int32)[:, None] == position[None, :]).astype(jnp.bfloat16)
    send = jnp.dot(placing, payload, preferred_element_type=jnp.float32).astype(jnp.bfloat16)
    width = 2 * length + extra
    got = lax.all_to_all(
        send.reshape(devices_all, capacity, width), ("slab", "grp"), split_axis=0, concat_axis=0, tiled=True
    ).reshape(slot_count, width)

    rows_in = got[:, : 2 * length]
    weight_in = got[:, 2 * length : 2 * length + planes]
    line_in = got[:, 2 * length + planes].astype(jnp.float32)
    line_grid = jnp.arange(lines_per, dtype=jnp.float32)[None, :, None]
    spread = jnp.where(
        line_in[None, None, :] == line_grid, weight_in.T[:, None, :], jnp.zeros((), jnp.bfloat16)
    ).reshape(planes * lines_per, slot_count)
    volume = jnp.dot(spread, rows_in, preferred_element_type=jnp.float32)

    inverse = np.concatenate(
        [
            np.concatenate([cosine_table, sine_table], axis=1),
            np.concatenate([-sine_table, cosine_table], axis=1),
        ],
        axis=0,
    )
    inverse_blocked = jnp.asarray(
        inverse.reshape(2 * length, 2, slab_count, x_block).transpose(2, 1, 3, 0).reshape(2 * length, 2 * length),
        jnp.float32,
    )
    along_x = lax.dot_general(
        inverse_blocked, volume, (((1,), (1,)), ((), ())), precision=high, preferred_element_type=jnp.float32
    )
    along_x = along_x.astype(jnp.bfloat16).reshape(slab_count, 2, x_block, planes, lines_per)
    pencil = lax.all_to_all(along_x, "slab", split_axis=0, concat_axis=0, tiled=True)

    lhs = pencil.transpose(2, 4, 0, 1, 3).reshape(x_block * lines_per, 2 * length)
    z_table = inverse.reshape(2, slab_count, planes, 2 * length).transpose(1, 0, 2, 3).reshape(2 * length, 2 * length)
    z_high, z_low = halves(z_table)
    parts = []
    for part in range(2):
        columns = slice(part * length, (part + 1) * length)
        flat = jnp.dot(lhs, z_high[:, columns], preferred_element_type=jnp.float32)
        flat = flat + jnp.dot(lhs, z_low[:, columns], preferred_element_type=jnp.float32)
        parts.append(flat.reshape(x_block, lines_per, length))
    result = jnp.stack(parts)
    return result


def solution(mesh):
    return jax.shard_map(
        local,
        mesh=mesh,
        in_specs=(
            P(("slab", "grp"), None, None),
            P(("slab", "grp"), None),
            P(("slab", "grp"), None, None),
            P(("slab", "grp"), None),
            P(("slab", "grp"), None, None),
        ),
        out_specs=P(None, "slab", "grp", None),
        check_vma=False,
    )
```

```python
import math

import jax
import jax.numpy as jnp
import ml_dtypes
import numpy as np
from jax import lax
from jax.sharding import PartitionSpec as P


def twiddles(length):
    index_grid = np.arange(length)
    phase_angle = (np.outer(index_grid, index_grid) % length) * (2.0 * np.pi / length)
    norm_scale = 1.0 / math.sqrt(length)
    return (np.cos(phase_angle) * norm_scale, np.sin(phase_angle) * norm_scale)


def halves(values):
    high = values.astype(ml_dtypes.bfloat16)
    low = (values - high.astype(np.float64)).astype(ml_dtypes.bfloat16)
    return jnp.asarray(high), jnp.asarray(low)


def local(images, crossing_row, crossing_dest, crossing_line, interp_weight):
    high = lax.Precision.HIGH
    length = images.shape[1]
    crossings = crossing_row.shape[1]
    slab_count = lax.axis_size("slab")
    group_count = lax.axis_size("grp")
    devices_all = slab_count * group_count
    planes = length // slab_count
    lines_per = length // group_count
    capacity = 2 * crossings // devices_all
    slot_count = devices_all * capacity
    x_block = length // slab_count
    cosine_table, sine_table = twiddles(length)

    image = images[0]
    forward_y = jnp.asarray(np.concatenate([cosine_table, -sine_table], axis=0), jnp.float32)
    along_y = jnp.dot(forward_y, image, precision=high, preferred_element_type=jnp.float32)
    from_real = jnp.asarray(np.concatenate([cosine_table, -sine_table], axis=1), jnp.float32)
    from_imag = jnp.asarray(np.concatenate([sine_table, cosine_table], axis=1), jnp.float32)
    spectra = jnp.dot(along_y[:length], from_real, precision=high, preferred_element_type=jnp.float32)
    spectra = spectra + jnp.dot(along_y[length:], from_imag, precision=high, preferred_element_type=jnp.float32)
    spectra_low = spectra.astype(jnp.bfloat16)

    row_hits = (crossing_row[0][:, None] == jnp.arange(length, dtype=jnp.int32)[None, :]).astype(
        jnp.bfloat16
    )
    slice_rows = jnp.dot(row_hits, spectra_low, preferred_element_type=jnp.float32).astype(jnp.bfloat16)
    extra = 128
    meta_grid = jnp.arange(extra, dtype=jnp.int32)[None, :]
    weight_place = jnp.asarray(np.eye(planes, extra), jnp.bfloat16)
    meta = jnp.dot(interp_weight[0], weight_place, preferred_element_type=jnp.float32)
    meta = meta + jnp.where(meta_grid == planes, crossing_line[0][:, None].astype(jnp.float32), 0.0)
    payload = jnp.concatenate([slice_rows, meta.astype(jnp.bfloat16)], axis=1)

    destination = crossing_dest[0, :, 0]
    onehot = (destination[:, None] == jnp.arange(devices_all, dtype=jnp.int32)[None, :]).astype(jnp.int32)
    earlier = jnp.cumsum(onehot, axis=0) - onehot
    slot_within = jnp.sum(earlier * onehot, axis=1)
    position = destination * capacity + slot_within
    placing = (jnp.arange(slot_count, dtype=jnp.int32)[:, None] == position[None, :]).astype(jnp.bfloat16)
    send = jnp.dot(placing, payload, preferred_element_type=jnp.float32).astype(jnp.bfloat16)
    width = 2 * length + extra
    got = lax.all_to_all(
        send.reshape(devices_all, capacity, width), ("slab", "grp"), split_axis=0, concat_axis=0, tiled=True
    ).reshape(slot_count, width)

    rows_in = got[:, : 2 * length]
    weight_in = got[:, 2 * length : 2 * length + planes]
    line_in = got[:, 2 * length + planes].astype(jnp.float32)
    chunks = 2
    chunk_lines = lines_per // chunks
    line_grid = jnp.arange(lines_per, dtype=jnp.float32).reshape(chunks, 1, chunk_lines, 1)
    spread = jnp.where(
        line_in[None, None, None, :] == line_grid, weight_in.T[None, :, None, :], jnp.zeros((), jnp.bfloat16)
    ).reshape(planes * lines_per, slot_count)
    volume = jnp.dot(spread, rows_in, preferred_element_type=jnp.float32)

    inverse = np.concatenate(
        [
            np.concatenate([cosine_table, sine_table], axis=1),
            np.concatenate([-sine_table, cosine_table], axis=1),
        ],
        axis=0,
    )
    inverse_blocked = jnp.asarray(
        inverse.reshape(2 * length, 2, slab_count, x_block).transpose(2, 1, 3, 0).reshape(2 * length, 2 * length),
        jnp.float32,
    )
    z_table = inverse.reshape(2, slab_count, planes, 2 * length).transpose(1, 0, 2, 3).reshape(2 * length, 2 * length)
    z_high, z_low = halves(z_table)
    chunk_rows = planes * chunk_lines
    outputs = []
    for chunk in range(chunks):
        along_x = lax.dot_general(
            inverse_blocked,
            volume[chunk * chunk_rows : (chunk + 1) * chunk_rows],
            (((1,), (1,)), ((), ())),
            precision=high,
            preferred_element_type=jnp.float32,
        )
        along_x = along_x.astype(jnp.bfloat16).reshape(slab_count, 2, x_block, planes, chunk_lines)
        pencil = lax.all_to_all(along_x, "slab", split_axis=0, concat_axis=0, tiled=True)
        lhs = pencil.transpose(2, 4, 0, 1, 3).reshape(x_block * chunk_lines, 2 * length)
        parts = []
        for part in range(2):
            columns = slice(part * length, (part + 1) * length)
            flat = jnp.dot(lhs, z_high[:, columns], preferred_element_type=jnp.float32)
            flat = flat + jnp.dot(lhs, z_low[:, columns], preferred_element_type=jnp.float32)
            parts.append(flat.reshape(x_block, chunk_lines, length))
        outputs.append(jnp.stack(parts))
    result = jnp.concatenate(outputs, axis=2)
    return result


def solution(mesh):
    return jax.shard_map(
        local,
        mesh=mesh,
        in_specs=(
            P(("slab", "grp"), None, None),
            P(("slab", "grp"), None),
            P(("slab", "grp"), None, None),
            P(("slab", "grp"), None),
            P(("slab", "grp"), None, None),
        ),
        out_specs=P(None, "slab", "grp", None),
        check_vma=False,
    )
```

```python
import math

import jax
import jax.numpy as jnp
import ml_dtypes
import numpy as np
from jax import lax
from jax.sharding import PartitionSpec as P


def twiddles(length):
    index_grid = np.arange(length)
    phase_angle = (np.outer(index_grid, index_grid) % length) * (2.0 * np.pi / length)
    norm_scale = 1.0 / math.sqrt(length)
    return (np.cos(phase_angle) * norm_scale, np.sin(phase_angle) * norm_scale)


def halves(values):
    high = values.astype(ml_dtypes.bfloat16)
    low = (values - high.astype(np.float64)).astype(ml_dtypes.bfloat16)
    return jnp.asarray(high), jnp.asarray(low)


def local(images, crossing_row, crossing_dest, crossing_line, interp_weight):
    high = lax.Precision.HIGH
    length = images.shape[1]
    crossings = crossing_row.shape[1]
    slab_count = lax.axis_size("slab")
    group_count = lax.axis_size("grp")
    devices_all = slab_count * group_count
    planes = length // slab_count
    lines_per = length // group_count
    capacity = 2 * crossings // devices_all
    slot_count = devices_all * capacity
    x_block = length // slab_count
    cosine_table, sine_table = twiddles(length)

    image = images[0]
    forward_y = jnp.asarray(np.concatenate([cosine_table, -sine_table], axis=0), jnp.float32)
    along_y = jnp.dot(forward_y, image, precision=high, preferred_element_type=jnp.float32)
    from_real = jnp.asarray(np.concatenate([cosine_table, -sine_table], axis=1), jnp.float32)
    from_imag = jnp.asarray(np.concatenate([sine_table, cosine_table], axis=1), jnp.float32)
    spectra = jnp.dot(along_y[:length], from_real, precision=high, preferred_element_type=jnp.float32)
    spectra = spectra + jnp.dot(along_y[length:], from_imag, precision=high, preferred_element_type=jnp.float32)
    spectra_low = spectra.astype(jnp.bfloat16)

    row_hits = (crossing_row[0][:, None] == jnp.arange(length, dtype=jnp.int32)[None, :]).astype(
        jnp.bfloat16
    )
    slice_rows = jnp.dot(row_hits, spectra_low, preferred_element_type=jnp.float32).astype(jnp.bfloat16)
    extra = 128
    meta_grid = jnp.arange(extra, dtype=jnp.int32)[None, :]
    weight_place = jnp.asarray(np.eye(planes, extra), jnp.bfloat16)
    meta = jnp.dot(interp_weight[0], weight_place, preferred_element_type=jnp.float32)
    meta = meta + jnp.where(meta_grid == planes, crossing_line[0][:, None].astype(jnp.float32), 0.0)
    payload = jnp.concatenate([slice_rows, meta.astype(jnp.bfloat16)], axis=1)

    destination = crossing_dest[0, :, 0]
    onehot = (destination[:, None] == jnp.arange(devices_all, dtype=jnp.int32)[None, :]).astype(jnp.int32)
    earlier = jnp.cumsum(onehot, axis=0) - onehot
    slot_within = jnp.sum(earlier * onehot, axis=1)
    position = destination * capacity + slot_within
    placing = (jnp.arange(slot_count, dtype=jnp.int32)[:, None] == position[None, :]).astype(jnp.bfloat16)
    send = jnp.dot(placing, payload, preferred_element_type=jnp.float32).astype(jnp.bfloat16)
    width = 2 * length + extra
    got = lax.all_to_all(
        send.reshape(devices_all, capacity, width), ("slab", "grp"), split_axis=0, concat_axis=0, tiled=True
    ).reshape(slot_count, width)

    rows_in = got[:, : 2 * length]
    weight_in = got[:, 2 * length : 2 * length + planes]
    line_in = got[:, 2 * length + planes].astype(jnp.float32)
    line_grid = jnp.arange(lines_per, dtype=jnp.float32)[None, :, None]
    spread = jnp.where(
        line_in[None, None, :] == line_grid, weight_in.T[:, None, :], jnp.zeros((), jnp.bfloat16)
    ).reshape(planes * lines_per, slot_count)
    volume = jnp.dot(spread, rows_in, preferred_element_type=jnp.float32)

    inverse = np.concatenate(
        [
            np.concatenate([cosine_table, sine_table], axis=1),
            np.concatenate([-sine_table, cosine_table], axis=1),
        ],
        axis=0,
    )
    chunks = 2
    chunk_x = x_block // chunks
    inverse_blocked = jnp.asarray(
        inverse.reshape(2 * length, 2, slab_count, chunks, chunk_x)
        .transpose(3, 2, 1, 4, 0)
        .reshape(2 * length, 2 * length),
        jnp.float32,
    )
    z_table = inverse.reshape(2, slab_count, planes, 2 * length).transpose(1, 0, 2, 3).reshape(2 * length, 2 * length)
    z_high, z_low = halves(z_table)
    chunk_rows = 2 * length // chunks
    outputs = []
    for chunk in range(chunks):
        along_x = lax.dot_general(
            inverse_blocked[chunk * chunk_rows : (chunk + 1) * chunk_rows],
            volume,
            (((1,), (1,)), ((), ())),
            precision=high,
            preferred_element_type=jnp.float32,
        )
        along_x = along_x.astype(jnp.bfloat16).reshape(slab_count, 2, chunk_x, planes, lines_per)
        pencil = lax.all_to_all(along_x, "slab", split_axis=0, concat_axis=0, tiled=True)
        lhs = pencil.transpose(2, 4, 0, 1, 3).reshape(chunk_x * lines_per, 2 * length)
        parts = []
        for part in range(2):
            columns = slice(part * length, (part + 1) * length)
            flat = jnp.dot(lhs, z_high[:, columns], preferred_element_type=jnp.float32)
            flat = flat + jnp.dot(lhs, z_low[:, columns], preferred_element_type=jnp.float32)
            parts.append(flat.reshape(chunk_x, lines_per, length))
        outputs.append(jnp.stack(parts))
    result = jnp.concatenate(outputs, axis=1)
    return result


def solution(mesh):
    return jax.shard_map(
        local,
        mesh=mesh,
        in_specs=(
            P(("slab", "grp"), None, None),
            P(("slab", "grp"), None),
            P(("slab", "grp"), None, None),
            P(("slab", "grp"), None),
            P(("slab", "grp"), None, None),
        ),
        out_specs=P(None, "slab", "grp", None),
        check_vma=False,
    )
```

```python
import math

import jax
import jax.numpy as jnp
from jax import lax
from jax.sharding import PartitionSpec as P


def table(length, rows, columns, quarter_turns):
    phase = (rows * columns) % length * 4 + quarter_turns * length
    angle = (phase % (4 * length)).astype(jnp.float32) * (math.pi / (2 * length))
    return jnp.cos(angle) * (1.0 / math.sqrt(length))


def halves(values):
    high = lax.reduce_precision(values, exponent_bits=8, mantissa_bits=7)
    low = (values - high).astype(jnp.bfloat16)
    return high.astype(jnp.bfloat16), low


def local(images, crossing_row, crossing_dest, crossing_line, interp_weight):
    high = lax.Precision.HIGH
    length = images.shape[1]
    crossings = crossing_row.shape[1]
    slab_count = lax.axis_size("slab")
    group_count = lax.axis_size("grp")
    devices_all = slab_count * group_count
    planes = length // slab_count
    lines_per = length // group_count
    capacity = 2 * crossings // devices_all
    slot_count = devices_all * capacity
    x_block = length // slab_count

    image = images[0]
    grid_a = lax.broadcasted_iota(jnp.int32, (2 * length, length), 0)
    grid_b = lax.broadcasted_iota(jnp.int32, (2 * length, length), 1)
    forward_y = table(length, grid_a % length, grid_b, grid_a // length)
    along_y = jnp.dot(forward_y, image, precision=high, preferred_element_type=jnp.float32)
    grid_a = lax.broadcasted_iota(jnp.int32, (length, 2 * length), 0)
    grid_b = lax.broadcasted_iota(jnp.int32, (length, 2 * length), 1)
    from_real = table(length, grid_a, grid_b % length, grid_b // length)
    from_imag = table(length, grid_a, grid_b % length, grid_b // length - 1)
    spectra = jnp.dot(along_y[:length], from_real, precision=high, preferred_element_type=jnp.float32)
    spectra = spectra + jnp.dot(along_y[length:], from_imag, precision=high, preferred_element_type=jnp.float32)
    spectra_low = spectra.astype(jnp.bfloat16)

    row_hits = (crossing_row[0][:, None] == jnp.arange(length, dtype=jnp.int32)[None, :]).astype(
        jnp.bfloat16
    )
    slice_rows = jnp.dot(row_hits, spectra_low, preferred_element_type=jnp.float32).astype(jnp.bfloat16)
    extra = 128
    meta_grid = jnp.arange(extra, dtype=jnp.int32)[None, :]
    weight_place = (lax.broadcasted_iota(jnp.int32, (planes, extra), 0) == lax.broadcasted_iota(jnp.int32, (planes, extra), 1)).astype(jnp.bfloat16)
    meta = jnp.dot(interp_weight[0], weight_place, preferred_element_type=jnp.float32)
    meta = meta + jnp.where(meta_grid == planes, crossing_line[0][:, None].astype(jnp.float32), 0.0)
    payload = jnp.concatenate([slice_rows, meta.astype(jnp.bfloat16)], axis=1)

    destination = crossing_dest[0, :, 0]
    onehot = (destination[:, None] == jnp.arange(devices_all, dtype=jnp.int32)[None, :]).astype(jnp.int32)
    earlier = jnp.cumsum(onehot, axis=0) - onehot
    slot_within = jnp.sum(earlier * onehot, axis=1)
    position = destination * capacity + slot_within
    placing = (jnp.arange(slot_count, dtype=jnp.int32)[:, None] == position[None, :]).astype(jnp.bfloat16)
    send = jnp.dot(placing, payload, preferred_element_type=jnp.float32).astype(jnp.bfloat16)
    width = 2 * length + extra
    got = lax.all_to_all(
        send.reshape(devices_all, capacity, width), ("slab", "grp"), split_axis=0, concat_axis=0, tiled=True
    ).reshape(slot_count, width)

    rows_in = got[:, : 2 * length]
    weight_in = got[:, 2 * length : 2 * length + planes]
    line_in = got[:, 2 * length + planes].astype(jnp.float32)
    line_grid = jnp.arange(lines_per, dtype=jnp.float32)[None, :, None]
    spread = jnp.where(
        line_in[None, None, :] == line_grid, weight_in.T[:, None, :], jnp.zeros((), jnp.bfloat16)
    ).reshape(planes * lines_per, slot_count)
    volume = jnp.dot(spread, rows_in, preferred_element_type=jnp.float32)

    out_row = lax.broadcasted_iota(jnp.int32, (2 * length, 2 * length), 0)
    in_col = lax.broadcasted_iota(jnp.int32, (2 * length, 2 * length), 1)
    out_part = (out_row // x_block) % 2
    out_x = (out_row // (2 * x_block)) * x_block + out_row % x_block
    inverse_blocked = table(length, in_col % length, out_x, in_col // length - out_part)
    along_x = lax.dot_general(
        inverse_blocked, volume, (((1,), (1,)), ((), ())), precision=high, preferred_element_type=jnp.float32
    )
    along_x = along_x.astype(jnp.bfloat16).reshape(slab_count, 2, x_block, planes, lines_per)
    along_x = along_x.transpose(0, 1, 3, 2, 4)
    pencil = lax.all_to_all(along_x, "slab", split_axis=0, concat_axis=0, tiled=True)

    lhs = pencil.transpose(3, 4, 0, 1, 2).reshape(x_block * lines_per, 2 * length)
    k_row = lax.broadcasted_iota(jnp.int32, (2 * length, 2 * length), 0)
    q_col = lax.broadcasted_iota(jnp.int32, (2 * length, 2 * length), 1)
    k_part = (k_row // planes) % 2
    k_z = (k_row // (2 * planes)) * planes + k_row % planes
    z_high, z_low = halves(table(length, k_z, q_col % length, k_part - q_col // length))
    parts = []
    for part in range(2):
        columns = slice(part * length, (part + 1) * length)
        flat = jnp.dot(lhs, z_high[:, columns], preferred_element_type=jnp.float32)
        flat = flat + jnp.dot(lhs, z_low[:, columns], preferred_element_type=jnp.float32)
        parts.append(flat.reshape(x_block, lines_per, length))
    result = jnp.stack(parts)
    return result


def solution(mesh):
    return jax.shard_map(
        local,
        mesh=mesh,
        in_specs=(
            P(("slab", "grp"), None, None),
            P(("slab", "grp"), None),
            P(("slab", "grp"), None, None),
            P(("slab", "grp"), None),
            P(("slab", "grp"), None, None),
        ),
        out_specs=P(None, "slab", "grp", None),
        check_vma=False,
    )
```

```python
import math

import jax
import jax.numpy as jnp
import ml_dtypes
import numpy as np
from jax import lax
from jax.experimental import pallas as pl
from jax.sharding import PartitionSpec as P


def twiddles(length):
    index_grid = np.arange(length)
    phase_angle = (np.outer(index_grid, index_grid) % length) * (2.0 * np.pi / length)
    norm_scale = 1.0 / math.sqrt(length)
    return (np.cos(phase_angle) * norm_scale, np.sin(phase_angle) * norm_scale)


def halves(values):
    high = values.astype(ml_dtypes.bfloat16)
    low = (values - high.astype(np.float64)).astype(ml_dtypes.bfloat16)
    return jnp.asarray(high), jnp.asarray(low)


def accumulate_and_transform(spread_ref, rows_ref, inverse_high_ref, inverse_low_ref, out_ref):
    volume = jnp.dot(spread_ref[...], rows_ref[...], preferred_element_type=jnp.float32)
    volume_high = volume.astype(jnp.bfloat16)
    volume_low = (volume - volume_high.astype(jnp.float32)).astype(jnp.bfloat16)
    contract = (((1,), (1,)), ((), ()))
    along = lax.dot_general(inverse_high_ref[...], volume_high, contract, preferred_element_type=jnp.float32)
    along = along + lax.dot_general(inverse_high_ref[...], volume_low, contract, preferred_element_type=jnp.float32)
    along = along + lax.dot_general(inverse_low_ref[...], volume_high, contract, preferred_element_type=jnp.float32)
    blocks, _, parts, x_in, lanes = out_ref.shape
    for part in range(parts):
        piece = along[:, part * lanes : (part + 1) * lanes].reshape(blocks, 2, x_in, lanes)
        out_ref[:, :, part, :, :] = piece.astype(out_ref.dtype)


def local(images, crossing_row, crossing_dest, crossing_line, interp_weight):
    high = lax.Precision.HIGH
    length = images.shape[1]
    crossings = crossing_row.shape[1]
    slab_count = lax.axis_size("slab")
    group_count = lax.axis_size("grp")
    devices_all = slab_count * group_count
    planes = length // slab_count
    lines_per = length // group_count
    capacity = 2 * crossings // devices_all
    slot_count = devices_all * capacity
    x_block = length // slab_count
    cosine_table, sine_table = twiddles(length)

    image = images[0]
    forward_y = jnp.asarray(np.concatenate([cosine_table, -sine_table], axis=0), jnp.float32)
    along_y = jnp.dot(forward_y, image, precision=high, preferred_element_type=jnp.float32)
    from_real = jnp.asarray(np.concatenate([cosine_table, -sine_table], axis=1), jnp.float32)
    from_imag = jnp.asarray(np.concatenate([sine_table, cosine_table], axis=1), jnp.float32)
    spectra = jnp.dot(along_y[:length], from_real, precision=high, preferred_element_type=jnp.float32)
    spectra = spectra + jnp.dot(along_y[length:], from_imag, precision=high, preferred_element_type=jnp.float32)
    spectra_low = spectra.astype(jnp.bfloat16)

    row_hits = (crossing_row[0][:, None] == jnp.arange(length, dtype=jnp.int32)[None, :]).astype(
        jnp.bfloat16
    )
    slice_rows = jnp.dot(row_hits, spectra_low, preferred_element_type=jnp.float32).astype(jnp.bfloat16)
    extra = 128
    meta_grid = jnp.arange(extra, dtype=jnp.int32)[None, :]
    weight_place = jnp.asarray(np.eye(planes, extra), jnp.bfloat16)
    meta = jnp.dot(interp_weight[0], weight_place, preferred_element_type=jnp.float32)
    meta = meta + jnp.where(meta_grid == planes, crossing_line[0][:, None].astype(jnp.float32), 0.0)
    payload = jnp.concatenate([slice_rows, meta.astype(jnp.bfloat16)], axis=1)

    destination = crossing_dest[0, :, 0]
    onehot = (destination[:, None] == jnp.arange(devices_all, dtype=jnp.int32)[None, :]).astype(jnp.int32)
    earlier = jnp.cumsum(onehot, axis=0) - onehot
    slot_within = jnp.sum(earlier * onehot, axis=1)
    position = destination * capacity + slot_within
    placing = (jnp.arange(slot_count, dtype=jnp.int32)[:, None] == position[None, :]).astype(jnp.bfloat16)
    send = jnp.dot(placing, payload, preferred_element_type=jnp.float32).astype(jnp.bfloat16)
    width = 2 * length + extra
    got = lax.all_to_all(
        send.reshape(devices_all, capacity, width), ("slab", "grp"), split_axis=0, concat_axis=0, tiled=True
    ).reshape(slot_count, width)

    weight_in = got[:, 2 * length : 2 * length + planes]
    line_in = got[:, 2 * length + planes].astype(jnp.float32)
    line_grid = jnp.arange(lines_per, dtype=jnp.float32)[None, :, None]
    spread = jnp.where(
        line_in[None, None, :] == line_grid, weight_in.T[:, None, :], jnp.zeros((), jnp.bfloat16)
    ).reshape(planes * lines_per, slot_count)

    inverse = np.concatenate(
        [
            np.concatenate([cosine_table, sine_table], axis=1),
            np.concatenate([-sine_table, cosine_table], axis=1),
        ],
        axis=0,
    )
    inverse_high, inverse_low = halves(
        inverse.reshape(2 * length, 2, slab_count, x_block).transpose(2, 1, 3, 0).reshape(2 * length, 2 * length)
    )
    step_planes = 2
    step_columns = step_planes * lines_per
    along_x = pl.pallas_call(
        accumulate_and_transform,
        out_shape=jax.ShapeDtypeStruct((slab_count, 2, planes, x_block, lines_per), jnp.bfloat16),
        grid=(planes // step_planes,),
        in_specs=[
            pl.BlockSpec((step_columns, slot_count), lambda i: (i, 0)),
            pl.BlockSpec((slot_count, 2 * length), lambda i: (0, 0)),
            pl.BlockSpec((2 * length, 2 * length), lambda i: (0, 0)),
            pl.BlockSpec((2 * length, 2 * length), lambda i: (0, 0)),
        ],
        out_specs=pl.BlockSpec((slab_count, 2, step_planes, x_block, lines_per), lambda i: (0, 0, i, 0, 0)),
    )(spread, got, inverse_high, inverse_low)
    pencil = lax.all_to_all(along_x, "slab", split_axis=0, concat_axis=0, tiled=True)

    lhs = pencil.transpose(3, 4, 0, 1, 2).reshape(x_block * lines_per, 2 * length)
    z_table = inverse.reshape(2, slab_count, planes, 2 * length).transpose(1, 0, 2, 3).reshape(2 * length, 2 * length)
    z_high, z_low = halves(z_table)
    parts = []
    for part in range(2):
        columns = slice(part * length, (part + 1) * length)
        flat = jnp.dot(lhs, z_high[:, columns], preferred_element_type=jnp.float32)
        flat = flat + jnp.dot(lhs, z_low[:, columns], preferred_element_type=jnp.float32)
        parts.append(flat.reshape(x_block, lines_per, length))
    result = jnp.stack(parts)
    return result


def solution(mesh):
    return jax.shard_map(
        local,
        mesh=mesh,
        in_specs=(
            P(("slab", "grp"), None, None),
            P(("slab", "grp"), None),
            P(("slab", "grp"), None, None),
            P(("slab", "grp"), None),
            P(("slab", "grp"), None, None),
        ),
        out_specs=P(None, "slab", "grp", None),
        check_vma=False,
    )
```

```python
import math

import jax
import jax.numpy as jnp
import ml_dtypes
import numpy as np
from jax import lax
from jax.experimental import pallas as pl
from jax.sharding import PartitionSpec as P


def twiddles(length):
    index_grid = np.arange(length)
    phase_angle = (np.outer(index_grid, index_grid) % length) * (2.0 * np.pi / length)
    norm_scale = 1.0 / math.sqrt(length)
    return (np.cos(phase_angle) * norm_scale, np.sin(phase_angle) * norm_scale)


def halves(values):
    high = values.astype(ml_dtypes.bfloat16)
    low = (values - high.astype(np.float64)).astype(ml_dtypes.bfloat16)
    return jnp.asarray(high), jnp.asarray(low)


def accumulate_and_transform(spread_ref, rows_ref, inverse_high_ref, inverse_low_ref, out_ref):
    volume = jnp.dot(spread_ref[...], rows_ref[...], preferred_element_type=jnp.float32)
    volume_high = volume.astype(jnp.bfloat16)
    volume_low = (volume - volume_high.astype(jnp.float32)).astype(jnp.bfloat16)
    contract = (((1,), (1,)), ((), ()))
    along = lax.dot_general(inverse_high_ref[...], volume_high, contract, preferred_element_type=jnp.float32)
    along = along + lax.dot_general(inverse_high_ref[...], volume_low, contract, preferred_element_type=jnp.float32)
    along = along + lax.dot_general(inverse_low_ref[...], volume_high, contract, preferred_element_type=jnp.float32)
    blocks, _, parts, x_in, lanes = out_ref.shape
    for part in range(parts):
        piece = along[:, part * lanes : (part + 1) * lanes].reshape(blocks, 2, x_in, lanes)
        out_ref[:, :, part, :, :] = piece.astype(out_ref.dtype)


def local(images, crossing_row, crossing_dest, crossing_line, interp_weight):
    high = lax.Precision.HIGH
    length = images.shape[1]
    crossings = crossing_row.shape[1]
    slab_count = lax.axis_size("slab")
    group_count = lax.axis_size("grp")
    devices_all = slab_count * group_count
    planes = length // slab_count
    lines_per = length // group_count
    capacity = 2 * crossings // devices_all
    slot_count = devices_all * capacity
    x_block = length // slab_count
    cosine_table, sine_table = twiddles(length)

    image = images[0]
    forward_y = jnp.asarray(np.concatenate([cosine_table, -sine_table], axis=0), jnp.float32)
    along_y = jnp.dot(forward_y, image, precision=high, preferred_element_type=jnp.float32)
    from_real = jnp.asarray(np.concatenate([cosine_table, -sine_table], axis=1), jnp.float32)
    from_imag = jnp.asarray(np.concatenate([sine_table, cosine_table], axis=1), jnp.float32)
    spectra = jnp.dot(along_y[:length], from_real, precision=high, preferred_element_type=jnp.float32)
    spectra = spectra + jnp.dot(along_y[length:], from_imag, precision=high, preferred_element_type=jnp.float32)
    spectra_low = spectra.astype(jnp.bfloat16)

    row_hits = (crossing_row[0][:, None] == jnp.arange(length, dtype=jnp.int32)[None, :]).astype(
        jnp.bfloat16
    )
    slice_rows = jnp.dot(row_hits, spectra_low, preferred_element_type=jnp.float32).astype(jnp.bfloat16)
    extra = 128
    meta_grid = jnp.arange(extra, dtype=jnp.int32)[None, :]
    weight_place = jnp.asarray(np.eye(planes, extra), jnp.bfloat16)
    meta = jnp.dot(interp_weight[0], weight_place, preferred_element_type=jnp.float32)
    meta = meta + jnp.where(meta_grid == planes, crossing_line[0][:, None].astype(jnp.float32), 0.0)
    payload = jnp.concatenate([slice_rows, meta.astype(jnp.bfloat16)], axis=1)

    destination = crossing_dest[0, :, 0]
    onehot = (destination[:, None] == jnp.arange(devices_all, dtype=jnp.int32)[None, :]).astype(jnp.int32)
    earlier = jnp.cumsum(onehot, axis=0) - onehot
    slot_within = jnp.sum(earlier * onehot, axis=1)
    position = destination * capacity + slot_within
    placing = (jnp.arange(slot_count, dtype=jnp.int32)[:, None] == position[None, :]).astype(jnp.bfloat16)
    send = jnp.dot(placing, payload, preferred_element_type=jnp.float32).astype(jnp.bfloat16)
    width = 2 * length + extra
    got = lax.all_to_all(
        send.reshape(devices_all, capacity, width), ("slab", "grp"), split_axis=0, concat_axis=0, tiled=True
    ).reshape(slot_count, width)

    weight_in = got[:, 2 * length : 2 * length + planes]
    line_in = got[:, 2 * length + planes].astype(jnp.float32)
    line_grid = jnp.arange(lines_per, dtype=jnp.float32)[None, :, None]
    spread = jnp.where(
        line_in[None, None, :] == line_grid, weight_in.T[:, None, :], jnp.zeros((), jnp.bfloat16)
    ).reshape(planes * lines_per, slot_count)

    inverse = np.concatenate(
        [
            np.concatenate([cosine_table, sine_table], axis=1),
            np.concatenate([-sine_table, cosine_table], axis=1),
        ],
        axis=0,
    )
    inverse_high, inverse_low = halves(
        inverse.reshape(2 * length, 2, slab_count, x_block).transpose(2, 1, 3, 0).reshape(2 * length, 2 * length)
    )
    step_planes = 2
    step_columns = step_planes * lines_per
    along_x = pl.pallas_call(
        accumulate_and_transform,
        out_shape=jax.ShapeDtypeStruct((slab_count, 2, planes, x_block, lines_per), jnp.bfloat16),
        grid=(planes // step_planes,),
        in_specs=[
            pl.BlockSpec((step_columns, slot_count), lambda i: (i, 0)),
            pl.BlockSpec((slot_count, 2 * length), lambda i: (0, 0)),
            pl.BlockSpec((2 * length, 2 * length), lambda i: (0, 0)),
            pl.BlockSpec((2 * length, 2 * length), lambda i: (0, 0)),
        ],
        out_specs=pl.BlockSpec((slab_count, 2, step_planes, x_block, lines_per), lambda i: (0, 0, i, 0, 0)),
    )(spread, got, inverse_high, inverse_low)
    pencil = lax.all_to_all(along_x, "slab", split_axis=0, concat_axis=0, tiled=True)

    lhs = pencil.transpose(3, 4, 0, 1, 2).reshape(x_block * lines_per, 2 * length)
    z_table = inverse.reshape(2, slab_count, planes, 2 * length).transpose(1, 0, 2, 3).reshape(2 * length, 2 * length)
    z_high, z_low = halves(z_table)
    z_high = z_high.reshape(2 * length, 2, length).transpose(1, 0, 2)
    z_low = z_low.reshape(2 * length, 2, length).transpose(1, 0, 2)
    both = jnp.broadcast_to(lhs[None], (2,) + lhs.shape)
    batched = (((2,), (1,)), ((0,), (0,)))
    flat = lax.dot_general(both, z_high, batched, preferred_element_type=jnp.float32)
    flat = flat + lax.dot_general(both, z_low, batched, preferred_element_type=jnp.float32)
    result = flat.reshape(2, x_block, lines_per, length)
    return result


def solution(mesh):
    return jax.shard_map(
        local,
        mesh=mesh,
        in_specs=(
            P(("slab", "grp"), None, None),
            P(("slab", "grp"), None),
            P(("slab", "grp"), None, None),
            P(("slab", "grp"), None),
            P(("slab", "grp"), None, None),
        ),
        out_specs=P(None, "slab", "grp", None),
        check_vma=False,
    )
```

```python
import math

import jax
import jax.numpy as jnp
import ml_dtypes
import numpy as np
from jax import lax
from jax.experimental import pallas as pl
from jax.sharding import PartitionSpec as P


def twiddles(length):
    index_grid = np.arange(length)
    phase_angle = (np.outer(index_grid, index_grid) % length) * (2.0 * np.pi / length)
    norm_scale = 1.0 / math.sqrt(length)
    return (np.cos(phase_angle) * norm_scale, np.sin(phase_angle) * norm_scale)


def halves(values):
    high = values.astype(ml_dtypes.bfloat16)
    low = (values - high.astype(np.float64)).astype(ml_dtypes.bfloat16)
    return jnp.asarray(high), jnp.asarray(low)


def accumulate_and_transform(weight_ref, line_ref, rows_ref, inverse_high_ref, inverse_low_ref, out_ref):
    weights = weight_ref[0]
    lines = out_ref.shape[-1]
    hit = line_ref[...] == lax.broadcasted_iota(jnp.int32, (lines, weights.shape[1]), 0)
    spread = jnp.concatenate(
        [jnp.where(hit, weights[plane : plane + 1, :], 0.0) for plane in range(weights.shape[0])], axis=0
    )
    volume = jnp.dot(spread.astype(jnp.bfloat16), rows_ref[...], preferred_element_type=jnp.float32)
    volume_high = volume.astype(jnp.bfloat16)
    volume_low = (volume - volume_high.astype(jnp.float32)).astype(jnp.bfloat16)
    contract = (((1,), (1,)), ((), ()))
    along = lax.dot_general(inverse_high_ref[...], volume_high, contract, preferred_element_type=jnp.float32)
    along = along + lax.dot_general(inverse_high_ref[...], volume_low, contract, preferred_element_type=jnp.float32)
    along = along + lax.dot_general(inverse_low_ref[...], volume_high, contract, preferred_element_type=jnp.float32)
    blocks, _, parts, x_in, lanes = out_ref.shape
    for part in range(parts):
        piece = along[:, part * lanes : (part + 1) * lanes].reshape(blocks, 2, x_in, lanes)
        out_ref[:, :, part, :, :] = piece.astype(out_ref.dtype)


def local(images, crossing_row, crossing_dest, crossing_line, interp_weight):
    high = lax.Precision.HIGH
    length = images.shape[1]
    crossings = crossing_row.shape[1]
    slab_count = lax.axis_size("slab")
    group_count = lax.axis_size("grp")
    devices_all = slab_count * group_count
    planes = length // slab_count
    lines_per = length // group_count
    capacity = 2 * crossings // devices_all
    slot_count = devices_all * capacity
    x_block = length // slab_count
    cosine_table, sine_table = twiddles(length)

    image = images[0]
    forward_y = jnp.asarray(np.concatenate([cosine_table, -sine_table], axis=0), jnp.float32)
    along_y = jnp.dot(forward_y, image, precision=high, preferred_element_type=jnp.float32)
    from_real = jnp.asarray(np.concatenate([cosine_table, -sine_table], axis=1), jnp.float32)
    from_imag = jnp.asarray(np.concatenate([sine_table, cosine_table], axis=1), jnp.float32)
    spectra = jnp.dot(along_y[:length], from_real, precision=high, preferred_element_type=jnp.float32)
    spectra = spectra + jnp.dot(along_y[length:], from_imag, precision=high, preferred_element_type=jnp.float32)
    spectra_low = spectra.astype(jnp.bfloat16)

    row_hits = (crossing_row[0][:, None] == jnp.arange(length, dtype=jnp.int32)[None, :]).astype(
        jnp.bfloat16
    )
    slice_rows = jnp.dot(row_hits, spectra_low, preferred_element_type=jnp.float32).astype(jnp.bfloat16)
    extra = 128
    meta_grid = jnp.arange(extra, dtype=jnp.int32)[None, :]
    weight_place = jnp.asarray(np.eye(planes, extra), jnp.bfloat16)
    meta = jnp.dot(interp_weight[0], weight_place, preferred_element_type=jnp.float32)
    meta = meta + jnp.where(meta_grid == planes, crossing_line[0][:, None].astype(jnp.float32), 0.0)
    payload = jnp.concatenate([slice_rows, meta.astype(jnp.bfloat16)], axis=1)

    destination = crossing_dest[0, :, 0]
    onehot = (destination[:, None] == jnp.arange(devices_all, dtype=jnp.int32)[None, :]).astype(jnp.int32)
    earlier = jnp.cumsum(onehot, axis=0) - onehot
    slot_within = jnp.sum(earlier * onehot, axis=1)
    position = destination * capacity + slot_within
    placing = (jnp.arange(slot_count, dtype=jnp.int32)[:, None] == position[None, :]).astype(jnp.bfloat16)
    send = jnp.dot(placing, payload, preferred_element_type=jnp.float32).astype(jnp.bfloat16)
    width = 2 * length + extra
    got = lax.all_to_all(
        send.reshape(devices_all, capacity, width), ("slab", "grp"), split_axis=0, concat_axis=0, tiled=True
    ).reshape(slot_count, width)

    step_planes = 2
    weight_in = (
        got[:, 2 * length : 2 * length + planes].T.astype(jnp.float32).reshape(planes // step_planes, step_planes, slot_count)
    )
    line_in = got[:, 2 * length + planes].astype(jnp.int32).reshape(1, slot_count)

    inverse = np.concatenate(
        [
            np.concatenate([cosine_table, sine_table], axis=1),
            np.concatenate([-sine_table, cosine_table], axis=1),
        ],
        axis=0,
    )
    inverse_high, inverse_low = halves(
        inverse.reshape(2 * length, 2, slab_count, x_block).transpose(2, 1, 3, 0).reshape(2 * length, 2 * length)
    )
    along_x = pl.pallas_call(
        accumulate_and_transform,
        out_shape=jax.ShapeDtypeStruct((slab_count, 2, planes, x_block, lines_per), jnp.bfloat16),
        grid=(planes // step_planes,),
        in_specs=[
            pl.BlockSpec((1, step_planes, slot_count), lambda i: (i, 0, 0)),
            pl.BlockSpec((1, slot_count), lambda i: (0, 0)),
            pl.BlockSpec((slot_count, 2 * length), lambda i: (0, 0)),
            pl.BlockSpec((2 * length, 2 * length), lambda i: (0, 0)),
            pl.BlockSpec((2 * length, 2 * length), lambda i: (0, 0)),
        ],
        out_specs=pl.BlockSpec((slab_count, 2, step_planes, x_block, lines_per), lambda i: (0, 0, i, 0, 0)),
    )(weight_in, line_in, got, inverse_high, inverse_low)
    pencil = lax.all_to_all(along_x, "slab", split_axis=0, concat_axis=0, tiled=True)

    lhs = pencil.transpose(3, 4, 0, 1, 2).reshape(x_block * lines_per, 2 * length)
    z_table = inverse.reshape(2, slab_count, planes, 2 * length).transpose(1, 0, 2, 3).reshape(2 * length, 2 * length)
    z_high, z_low = halves(z_table)
    parts = []
    for part in range(2):
        columns = slice(part * length, (part + 1) * length)
        flat = jnp.dot(lhs, z_high[:, columns], preferred_element_type=jnp.float32)
        flat = flat + jnp.dot(lhs, z_low[:, columns], preferred_element_type=jnp.float32)
        parts.append(flat.reshape(x_block, lines_per, length))
    result = jnp.stack(parts)
    return result


def solution(mesh):
    return jax.shard_map(
        local,
        mesh=mesh,
        in_specs=(
            P(("slab", "grp"), None, None),
            P(("slab", "grp"), None),
            P(("slab", "grp"), None, None),
            P(("slab", "grp"), None),
            P(("slab", "grp"), None, None),
        ),
        out_specs=P(None, "slab", "grp", None),
        check_vma=False,
    )
```

```python
import math

import jax
import jax.numpy as jnp
import ml_dtypes
import numpy as np
from jax import lax
from jax.experimental import pallas as pl
from jax.sharding import PartitionSpec as P


def twiddles(length):
    index_grid = np.arange(length)
    phase_angle = (np.outer(index_grid, index_grid) % length) * (2.0 * np.pi / length)
    norm_scale = 1.0 / math.sqrt(length)
    return (np.cos(phase_angle) * norm_scale, np.sin(phase_angle) * norm_scale)


def halves(values):
    high = values.astype(ml_dtypes.bfloat16)
    low = (values - high.astype(np.float64)).astype(ml_dtypes.bfloat16)
    return jnp.asarray(high), jnp.asarray(low)


def accumulate_and_transform(weight_ref, line_ref, rows_ref, inverse_high_ref, inverse_low_ref, out_ref):
    weights = weight_ref[0]
    lines = out_ref.shape[-1]
    hit = line_ref[...] == lax.broadcasted_iota(jnp.int32, (lines, weights.shape[1]), 0)
    spread = jnp.concatenate(
        [jnp.where(hit, weights[plane : plane + 1, :], 0.0) for plane in range(weights.shape[0])], axis=0
    )
    volume = jnp.dot(spread.astype(jnp.bfloat16), rows_ref[...], preferred_element_type=jnp.float32)
    volume_high = volume.astype(jnp.bfloat16)
    volume_low = (volume - volume_high.astype(jnp.float32)).astype(jnp.bfloat16)
    contract = (((1,), (1,)), ((), ()))
    along = lax.dot_general(inverse_high_ref[...], volume_high, contract, preferred_element_type=jnp.float32)
    along = along + lax.dot_general(inverse_high_ref[...], volume_low, contract, preferred_element_type=jnp.float32)
    along = along + lax.dot_general(inverse_low_ref[...], volume_high, contract, preferred_element_type=jnp.float32)
    blocks, _, parts, x_in, lanes = out_ref.shape
    for part in range(parts):
        piece = along[:, part * lanes : (part + 1) * lanes].reshape(blocks, 2, x_in, lanes)
        out_ref[:, :, part, :, :] = piece.astype(out_ref.dtype)


def along_z(lhs_ref, z_high_ref, z_low_ref, out_ref):
    rows = lhs_ref[...]
    total = jnp.dot(rows, z_high_ref[...], preferred_element_type=jnp.float32)
    total = total + jnp.dot(rows, z_low_ref[...], preferred_element_type=jnp.float32)
    length = out_ref.shape[-1]
    out_ref[0, 0] = total[:, :length]
    out_ref[1, 0] = total[:, length:]


def local(images, crossing_row, crossing_dest, crossing_line, interp_weight):
    high = lax.Precision.HIGH
    length = images.shape[1]
    crossings = crossing_row.shape[1]
    slab_count = lax.axis_size("slab")
    group_count = lax.axis_size("grp")
    devices_all = slab_count * group_count
    planes = length // slab_count
    lines_per = length // group_count
    capacity = 2 * crossings // devices_all
    slot_count = devices_all * capacity
    x_block = length // slab_count
    cosine_table, sine_table = twiddles(length)

    image = images[0]
    forward_y = jnp.asarray(np.concatenate([cosine_table, -sine_table], axis=0), jnp.float32)
    along_y = jnp.dot(forward_y, image, precision=high, preferred_element_type=jnp.float32)
    from_real = jnp.asarray(np.concatenate([cosine_table, -sine_table], axis=1), jnp.float32)
    from_imag = jnp.asarray(np.concatenate([sine_table, cosine_table], axis=1), jnp.float32)
    spectra = jnp.dot(along_y[:length], from_real, precision=high, preferred_element_type=jnp.float32)
    spectra = spectra + jnp.dot(along_y[length:], from_imag, precision=high, preferred_element_type=jnp.float32)
    spectra_low = spectra.astype(jnp.bfloat16)

    row_hits = (crossing_row[0][:, None] == jnp.arange(length, dtype=jnp.int32)[None, :]).astype(
        jnp.bfloat16
    )
    slice_rows = jnp.dot(row_hits, spectra_low, preferred_element_type=jnp.float32).astype(jnp.bfloat16)
    extra = 128
    meta_grid = jnp.arange(extra, dtype=jnp.int32)[None, :]
    weight_place = jnp.asarray(np.eye(planes, extra), jnp.bfloat16)
    meta = jnp.dot(interp_weight[0], weight_place, preferred_element_type=jnp.float32)
    meta = meta + jnp.where(meta_grid == planes, crossing_line[0][:, None].astype(jnp.float32), 0.0)
    payload = jnp.concatenate([slice_rows, meta.astype(jnp.bfloat16)], axis=1)

    destination = crossing_dest[0, :, 0]
    onehot = (destination[:, None] == jnp.arange(devices_all, dtype=jnp.int32)[None, :]).astype(jnp.int32)
    earlier = jnp.cumsum(onehot, axis=0) - onehot
    slot_within = jnp.sum(earlier * onehot, axis=1)
    position = destination * capacity + slot_within
    placing = (jnp.arange(slot_count, dtype=jnp.int32)[:, None] == position[None, :]).astype(jnp.bfloat16)
    send = jnp.dot(placing, payload, preferred_element_type=jnp.float32).astype(jnp.bfloat16)
    width = 2 * length + extra
    got = lax.all_to_all(
        send.reshape(devices_all, capacity, width), ("slab", "grp"), split_axis=0, concat_axis=0, tiled=True
    ).reshape(slot_count, width)

    step_planes = 2
    weight_in = (
        got[:, 2 * length : 2 * length + planes].T.astype(jnp.float32).reshape(planes // step_planes, step_planes, slot_count)
    )
    line_in = got[:, 2 * length + planes].astype(jnp.int32).reshape(1, slot_count)

    inverse = np.concatenate(
        [
            np.concatenate([cosine_table, sine_table], axis=1),
            np.concatenate([-sine_table, cosine_table], axis=1),
        ],
        axis=0,
    )
    inverse_high, inverse_low = halves(
        inverse.reshape(2 * length, 2, slab_count, x_block).transpose(2, 1, 3, 0).reshape(2 * length, 2 * length)
    )
    along_x = pl.pallas_call(
        accumulate_and_transform,
        out_shape=jax.ShapeDtypeStruct((slab_count, 2, planes, x_block, lines_per), jnp.bfloat16),
        grid=(planes // step_planes,),
        in_specs=[
            pl.BlockSpec((1, step_planes, slot_count), lambda i: (i, 0, 0)),
            pl.BlockSpec((1, slot_count), lambda i: (0, 0)),
            pl.BlockSpec((slot_count, 2 * length), lambda i: (0, 0)),
            pl.BlockSpec((2 * length, 2 * length), lambda i: (0, 0)),
            pl.BlockSpec((2 * length, 2 * length), lambda i: (0, 0)),
        ],
        out_specs=pl.BlockSpec((slab_count, 2, step_planes, x_block, lines_per), lambda i: (0, 0, i, 0, 0)),
    )(weight_in, line_in, got, inverse_high, inverse_low)
    pencil = lax.all_to_all(along_x, "slab", split_axis=0, concat_axis=0, tiled=True)

    lhs = pencil.transpose(3, 4, 0, 1, 2).reshape(x_block * lines_per, 2 * length)
    z_table = inverse.reshape(2, slab_count, planes, 2 * length).transpose(1, 0, 2, 3).reshape(2 * length, 2 * length)
    z_high, z_low = halves(z_table)
    result = pl.pallas_call(
        along_z,
        out_shape=jax.ShapeDtypeStruct((2, x_block, lines_per, length), jnp.float32),
        grid=(x_block,),
        in_specs=[
            pl.BlockSpec((lines_per, 2 * length), lambda i: (i, 0)),
            pl.BlockSpec((2 * length, 2 * length), lambda i: (0, 0)),
            pl.BlockSpec((2 * length, 2 * length), lambda i: (0, 0)),
        ],
        out_specs=pl.BlockSpec((2, 1, lines_per, length), lambda i: (0, i, 0, 0)),
    )(lhs, z_high, z_low)
    return result


def solution(mesh):
    return jax.shard_map(
        local,
        mesh=mesh,
        in_specs=(
            P(("slab", "grp"), None, None),
            P(("slab", "grp"), None),
            P(("slab", "grp"), None, None),
            P(("slab", "grp"), None),
            P(("slab", "grp"), None, None),
        ),
        out_specs=P(None, "slab", "grp", None),
        check_vma=False,
    )
```

```python
import math

import jax
import jax.numpy as jnp
import ml_dtypes
import numpy as np
from jax import lax
from jax.experimental import pallas as pl
from jax.sharding import PartitionSpec as P


def twiddles(length):
    index_grid = np.arange(length)
    phase_angle = (np.outer(index_grid, index_grid) % length) * (2.0 * np.pi / length)
    norm_scale = 1.0 / math.sqrt(length)
    return (np.cos(phase_angle) * norm_scale, np.sin(phase_angle) * norm_scale)


def halves(values):
    high = values.astype(ml_dtypes.bfloat16)
    low = (values - high.astype(np.float64)).astype(ml_dtypes.bfloat16)
    return jnp.asarray(high), jnp.asarray(low)


def accumulate_and_transform(weight_ref, line_ref, rows_ref, inverse_high_ref, inverse_low_ref, out_ref):
    weights = weight_ref[0]
    lines = out_ref.shape[-1]
    hit = line_ref[...] == lax.broadcasted_iota(jnp.int32, (lines, weights.shape[1]), 0)
    spread = jnp.concatenate(
        [jnp.where(hit, weights[plane : plane + 1, :], 0.0) for plane in range(weights.shape[0])], axis=0
    )
    volume = jnp.dot(spread.astype(jnp.bfloat16), rows_ref[...], preferred_element_type=jnp.float32)
    volume_high = volume.astype(jnp.bfloat16)
    volume_low = (volume - volume_high.astype(jnp.float32)).astype(jnp.bfloat16)
    contract = (((1,), (1,)), ((), ()))
    along = lax.dot_general(inverse_high_ref[...], volume_high, contract, preferred_element_type=jnp.float32)
    along = along + lax.dot_general(inverse_high_ref[...], volume_low, contract, preferred_element_type=jnp.float32)
    along = along + lax.dot_general(inverse_low_ref[...], volume_high, contract, preferred_element_type=jnp.float32)
    blocks, _, parts, x_in, lanes = out_ref.shape
    for part in range(parts):
        piece = along[:, part * lanes : (part + 1) * lanes].reshape(blocks, 2, x_in, lanes)
        out_ref[:, :, part, :, :] = piece.astype(out_ref.dtype)


def along_z(z_high_ref, z_low_ref, pencil_ref, out_ref):
    columns = pencil_ref[...]
    total = jnp.dot(z_high_ref[...], columns, preferred_element_type=jnp.float32)
    total = total + jnp.dot(z_low_ref[...], columns, preferred_element_type=jnp.float32)
    _, xs, lines, length = out_ref.shape
    for part in range(2):
        for x in range(xs):
            out_ref[part, x] = total[part * length : (part + 1) * length, x * lines : (x + 1) * lines].T


def local(images, crossing_row, crossing_dest, crossing_line, interp_weight):
    high = lax.Precision.HIGH
    length = images.shape[1]
    crossings = crossing_row.shape[1]
    slab_count = lax.axis_size("slab")
    group_count = lax.axis_size("grp")
    devices_all = slab_count * group_count
    planes = length // slab_count
    lines_per = length // group_count
    capacity = 2 * crossings // devices_all
    slot_count = devices_all * capacity
    x_block = length // slab_count
    cosine_table, sine_table = twiddles(length)

    image = images[0]
    forward_y = jnp.asarray(np.concatenate([cosine_table, -sine_table], axis=0), jnp.float32)
    along_y = jnp.dot(forward_y, image, precision=high, preferred_element_type=jnp.float32)
    from_real = jnp.asarray(np.concatenate([cosine_table, -sine_table], axis=1), jnp.float32)
    from_imag = jnp.asarray(np.concatenate([sine_table, cosine_table], axis=1), jnp.float32)
    spectra = jnp.dot(along_y[:length], from_real, precision=high, preferred_element_type=jnp.float32)
    spectra = spectra + jnp.dot(along_y[length:], from_imag, precision=high, preferred_element_type=jnp.float32)
    spectra_low = spectra.astype(jnp.bfloat16)

    row_hits = (crossing_row[0][:, None] == jnp.arange(length, dtype=jnp.int32)[None, :]).astype(
        jnp.bfloat16
    )
    slice_rows = jnp.dot(row_hits, spectra_low, preferred_element_type=jnp.float32).astype(jnp.bfloat16)
    extra = 128
    meta_grid = jnp.arange(extra, dtype=jnp.int32)[None, :]
    weight_place = jnp.asarray(np.eye(planes, extra), jnp.bfloat16)
    meta = jnp.dot(interp_weight[0], weight_place, preferred_element_type=jnp.float32)
    meta = meta + jnp.where(meta_grid == planes, crossing_line[0][:, None].astype(jnp.float32), 0.0)
    payload = jnp.concatenate([slice_rows, meta.astype(jnp.bfloat16)], axis=1)

    destination = crossing_dest[0, :, 0]
    onehot = (destination[:, None] == jnp.arange(devices_all, dtype=jnp.int32)[None, :]).astype(jnp.int32)
    earlier = jnp.cumsum(onehot, axis=0) - onehot
    slot_within = jnp.sum(earlier * onehot, axis=1)
    position = destination * capacity + slot_within
    placing = (jnp.arange(slot_count, dtype=jnp.int32)[:, None] == position[None, :]).astype(jnp.bfloat16)
    send = jnp.dot(placing, payload, preferred_element_type=jnp.float32).astype(jnp.bfloat16)
    width = 2 * length + extra
    got = lax.all_to_all(
        send.reshape(devices_all, capacity, width), ("slab", "grp"), split_axis=0, concat_axis=0, tiled=True
    ).reshape(slot_count, width)

    step_planes = 2
    weight_in = (
        got[:, 2 * length : 2 * length + planes].T.astype(jnp.float32).reshape(planes // step_planes, step_planes, slot_count)
    )
    line_in = got[:, 2 * length + planes].astype(jnp.int32).reshape(1, slot_count)

    inverse = np.concatenate(
        [
            np.concatenate([cosine_table, sine_table], axis=1),
            np.concatenate([-sine_table, cosine_table], axis=1),
        ],
        axis=0,
    )
    inverse_high, inverse_low = halves(
        inverse.reshape(2 * length, 2, slab_count, x_block).transpose(2, 1, 3, 0).reshape(2 * length, 2 * length)
    )
    along_x = pl.pallas_call(
        accumulate_and_transform,
        out_shape=jax.ShapeDtypeStruct((slab_count, 2, planes, x_block, lines_per), jnp.bfloat16),
        grid=(planes // step_planes,),
        in_specs=[
            pl.BlockSpec((1, step_planes, slot_count), lambda i: (i, 0, 0)),
            pl.BlockSpec((1, slot_count), lambda i: (0, 0)),
            pl.BlockSpec((slot_count, 2 * length), lambda i: (0, 0)),
            pl.BlockSpec((2 * length, 2 * length), lambda i: (0, 0)),
            pl.BlockSpec((2 * length, 2 * length), lambda i: (0, 0)),
        ],
        out_specs=pl.BlockSpec((slab_count, 2, step_planes, x_block, lines_per), lambda i: (0, 0, i, 0, 0)),
    )(weight_in, line_in, got, inverse_high, inverse_low)
    pencil = lax.all_to_all(along_x, "slab", split_axis=0, concat_axis=0, tiled=True)

    columns = pencil.reshape(2 * length, x_block * lines_per)
    z_table = inverse.reshape(2, slab_count, planes, 2 * length).transpose(1, 0, 2, 3).reshape(2 * length, 2 * length)
    z_high, z_low = halves(z_table.T)
    step_x = 2
    result = pl.pallas_call(
        along_z,
        out_shape=jax.ShapeDtypeStruct((2, x_block, lines_per, length), jnp.float32),
        grid=(x_block // step_x,),
        in_specs=[
            pl.BlockSpec((2 * length, 2 * length), lambda i: (0, 0)),
            pl.BlockSpec((2 * length, 2 * length), lambda i: (0, 0)),
            pl.BlockSpec((2 * length, step_x * lines_per), lambda i: (0, i)),
        ],
        out_specs=pl.BlockSpec((2, step_x, lines_per, length), lambda i: (0, i, 0, 0)),
    )(z_high, z_low, columns)
    return result


def solution(mesh):
    return jax.shard_map(
        local,
        mesh=mesh,
        in_specs=(
            P(("slab", "grp"), None, None),
            P(("slab", "grp"), None),
            P(("slab", "grp"), None, None),
            P(("slab", "grp"), None),
            P(("slab", "grp"), None, None),
        ),
        out_specs=P(None, "slab", "grp", None),
        check_vma=False,
    )
```

```python
import math

import jax
import jax.numpy as jnp
import ml_dtypes
import numpy as np
from jax import lax
from jax.experimental import pallas as pl
from jax.sharding import PartitionSpec as P


def twiddles(length):
    index_grid = np.arange(length)
    phase_angle = (np.outer(index_grid, index_grid) % length) * (2.0 * np.pi / length)
    norm_scale = 1.0 / math.sqrt(length)
    return (np.cos(phase_angle) * norm_scale, np.sin(phase_angle) * norm_scale)


def halves(values):
    high = values.astype(ml_dtypes.bfloat16)
    low = (values - high.astype(np.float64)).astype(ml_dtypes.bfloat16)
    return jnp.asarray(high), jnp.asarray(low)


def accumulate_and_transform(weight_ref, line_ref, rows_ref, inverse_high_ref, inverse_low_ref, out_ref):
    weights = weight_ref[0]
    lines = out_ref.shape[-1]
    hit = line_ref[...] == lax.broadcasted_iota(jnp.int32, (lines, weights.shape[1]), 0)
    spread = jnp.concatenate(
        [jnp.where(hit, weights[plane : plane + 1, :], 0.0) for plane in range(weights.shape[0])], axis=0
    )
    volume = jnp.dot(spread.astype(jnp.bfloat16), rows_ref[...], preferred_element_type=jnp.float32)
    volume_high = volume.astype(jnp.bfloat16)
    volume_low = (volume - volume_high.astype(jnp.float32)).astype(jnp.bfloat16)
    contract = (((1,), (1,)), ((), ()))
    along = lax.dot_general(inverse_high_ref[...], volume_high, contract, preferred_element_type=jnp.float32)
    along = along + lax.dot_general(inverse_high_ref[...], volume_low, contract, preferred_element_type=jnp.float32)
    along = along + lax.dot_general(inverse_low_ref[...], volume_high, contract, preferred_element_type=jnp.float32)
    blocks, _, parts, x_in, lanes = out_ref.shape
    for part in range(parts):
        piece = along[:, part * lanes : (part + 1) * lanes].reshape(blocks, 2, x_in, lanes)
        out_ref[:, :, part, :, :] = piece.astype(out_ref.dtype)


def local(images, crossing_row, crossing_dest, crossing_line, interp_weight):
    high = lax.Precision.HIGH
    length = images.shape[1]
    crossings = crossing_row.shape[1]
    slab_count = lax.axis_size("slab")
    group_count = lax.axis_size("grp")
    devices_all = slab_count * group_count
    planes = length // slab_count
    lines_per = length // group_count
    capacity = 2 * crossings // devices_all
    slot_count = devices_all * capacity
    x_block = length // slab_count
    cosine_table, sine_table = twiddles(length)

    image = images[0]
    forward_y = jnp.asarray(np.concatenate([cosine_table, -sine_table], axis=0), jnp.float32)
    along_y = jnp.dot(forward_y, image, precision=high, preferred_element_type=jnp.float32)
    from_real = jnp.asarray(np.concatenate([cosine_table, -sine_table], axis=1), jnp.float32)
    from_imag = jnp.asarray(np.concatenate([sine_table, cosine_table], axis=1), jnp.float32)
    spectra = jnp.dot(along_y[:length], from_real, precision=high, preferred_element_type=jnp.float32)
    spectra = spectra + jnp.dot(along_y[length:], from_imag, precision=high, preferred_element_type=jnp.float32)
    spectra_low = spectra.astype(jnp.bfloat16)

    row_hits = (crossing_row[0][:, None] == jnp.arange(length, dtype=jnp.int32)[None, :]).astype(
        jnp.bfloat16
    )
    slice_rows = jnp.dot(row_hits, spectra_low, preferred_element_type=jnp.float32).astype(jnp.bfloat16)
    extra = 128
    meta_grid = jnp.arange(extra, dtype=jnp.int32)[None, :]
    weight_place = jnp.asarray(np.eye(planes, extra), jnp.bfloat16)
    meta = jnp.dot(interp_weight[0], weight_place, preferred_element_type=jnp.float32)
    meta = meta + jnp.where(meta_grid == planes, crossing_line[0][:, None].astype(jnp.float32), 0.0)
    payload = jnp.concatenate([slice_rows, meta.astype(jnp.bfloat16)], axis=1)

    destination = crossing_dest[0, :, 0]
    onehot = (destination[:, None] == jnp.arange(devices_all, dtype=jnp.int32)[None, :]).astype(jnp.int32)
    earlier = jnp.cumsum(onehot, axis=0) - onehot
    slot_within = jnp.sum(earlier * onehot, axis=1)
    position = destination * capacity + slot_within
    placing = (jnp.arange(slot_count, dtype=jnp.int32)[:, None] == position[None, :]).astype(jnp.bfloat16)
    send = jnp.dot(placing, payload, preferred_element_type=jnp.float32).astype(jnp.bfloat16)
    width = 2 * length + extra
    got = lax.all_to_all(
        send.reshape(devices_all, capacity, width), ("slab", "grp"), split_axis=0, concat_axis=0, tiled=True
    ).reshape(slot_count, width)

    step_planes = 2
    weight_in = (
        got[:, 2 * length : 2 * length + planes].T.astype(jnp.float32).reshape(planes // step_planes, step_planes, slot_count)
    )
    line_in = got[:, 2 * length + planes].astype(jnp.int32).reshape(1, slot_count)

    inverse = np.concatenate(
        [
            np.concatenate([cosine_table, sine_table], axis=1),
            np.concatenate([-sine_table, cosine_table], axis=1),
        ],
        axis=0,
    )
    inverse_high, inverse_low = halves(
        inverse.reshape(2 * length, 2, slab_count, x_block).transpose(2, 1, 3, 0).reshape(2 * length, 2 * length)
    )
    along_x = pl.pallas_call(
        accumulate_and_transform,
        out_shape=jax.ShapeDtypeStruct((slab_count, 2, planes, x_block, lines_per), jnp.bfloat16),
        grid=(planes // step_planes,),
        in_specs=[
            pl.BlockSpec((1, step_planes, slot_count), lambda i: (i, 0, 0)),
            pl.BlockSpec((1, slot_count), lambda i: (0, 0)),
            pl.BlockSpec((slot_count, 2 * length), lambda i: (0, 0)),
            pl.BlockSpec((2 * length, 2 * length), lambda i: (0, 0)),
            pl.BlockSpec((2 * length, 2 * length), lambda i: (0, 0)),
        ],
        out_specs=pl.BlockSpec((slab_count, 2, step_planes, x_block, lines_per), lambda i: (0, 0, i, 0, 0)),
    )(weight_in, line_in, got, inverse_high, inverse_low)
    pencil = lax.all_to_all(along_x, "slab", split_axis=0, concat_axis=0, tiled=True)

    lhs = pencil.transpose(3, 4, 0, 1, 2).reshape(x_block * lines_per, 2 * length)
    z_table = inverse.reshape(2, slab_count, planes, 2 * length).transpose(1, 0, 2, 3).reshape(2 * length, 2 * length)
    z_high, z_low = halves(z_table)
    parts = []
    for part in range(2):
        columns = slice(part * length, (part + 1) * length)
        flat = jnp.dot(lhs, z_high[:, columns], preferred_element_type=jnp.float32)
        flat = flat + jnp.dot(lhs, z_low[:, columns], preferred_element_type=jnp.float32)
        parts.append(flat.reshape(1, x_block, lines_per, length))
    result = lax.dynamic_update_slice(
        jnp.broadcast_to(parts[0], (2, x_block, lines_per, length)), parts[1], (1, 0, 0, 0)
    )
    return result


def solution(mesh):
    return jax.shard_map(
        local,
        mesh=mesh,
        in_specs=(
            P(("slab", "grp"), None, None),
            P(("slab", "grp"), None),
            P(("slab", "grp"), None, None),
            P(("slab", "grp"), None),
            P(("slab", "grp"), None, None),
        ),
        out_specs=P(None, "slab", "grp", None),
        check_vma=False,
    )
```

```python
import math

import jax
import jax.numpy as jnp
import ml_dtypes
import numpy as np
from jax import lax
from jax.experimental import pallas as pl
from jax.sharding import PartitionSpec as P


def twiddles(length):
    index_grid = np.arange(length)
    phase_angle = (np.outer(index_grid, index_grid) % length) * (2.0 * np.pi / length)
    norm_scale = 1.0 / math.sqrt(length)
    return (np.cos(phase_angle) * norm_scale, np.sin(phase_angle) * norm_scale)


def halves(values):
    high = values.astype(ml_dtypes.bfloat16)
    low = (values - high.astype(np.float64)).astype(ml_dtypes.bfloat16)
    return jnp.asarray(high), jnp.asarray(low)


def accumulate_and_transform(weight_ref, line_ref, rows_ref, inverse_high_ref, inverse_low_ref, out_ref):
    weights = weight_ref[0]
    lines = out_ref.shape[-1]
    hit = line_ref[...] == lax.broadcasted_iota(jnp.int32, (lines, weights.shape[1]), 0)
    spread = jnp.concatenate(
        [jnp.where(hit, weights[plane : plane + 1, :], 0.0) for plane in range(weights.shape[0])], axis=0
    )
    volume = jnp.dot(spread.astype(jnp.bfloat16), rows_ref[...], preferred_element_type=jnp.float32)
    volume_high = volume.astype(jnp.bfloat16)
    volume_low = (volume - volume_high.astype(jnp.float32)).astype(jnp.bfloat16)
    contract = (((1,), (1,)), ((), ()))
    along = lax.dot_general(inverse_high_ref[...], volume_high, contract, preferred_element_type=jnp.float32)
    along = along + lax.dot_general(inverse_high_ref[...], volume_low, contract, preferred_element_type=jnp.float32)
    along = along + lax.dot_general(inverse_low_ref[...], volume_high, contract, preferred_element_type=jnp.float32)
    blocks, _, parts, x_in, lanes = out_ref.shape
    for part in range(parts):
        piece = along[:, part * lanes : (part + 1) * lanes].reshape(blocks, 2, x_in, lanes)
        out_ref[:, :, part, :, :] = piece.astype(out_ref.dtype)


def local(images, crossing_row, crossing_dest, crossing_line, interp_weight):
    high = lax.Precision.HIGH
    length = images.shape[1]
    crossings = crossing_row.shape[1]
    slab_count = lax.axis_size("slab")
    group_count = lax.axis_size("grp")
    devices_all = slab_count * group_count
    planes = length // slab_count
    lines_per = length // group_count
    capacity = 2 * crossings // devices_all
    slot_count = devices_all * capacity
    x_block = length // slab_count
    cosine_table, sine_table = twiddles(length)

    image = images[0]
    forward_y = jnp.asarray(np.concatenate([cosine_table, -sine_table], axis=0), jnp.float32)
    along_y = jnp.dot(forward_y, image, precision=high, preferred_element_type=jnp.float32)
    from_real = jnp.asarray(np.concatenate([cosine_table, -sine_table], axis=1), jnp.float32)
    from_imag = jnp.asarray(np.concatenate([sine_table, cosine_table], axis=1), jnp.float32)
    spectra = jnp.dot(along_y[:length], from_real, precision=high, preferred_element_type=jnp.float32)
    spectra = spectra + jnp.dot(along_y[length:], from_imag, precision=high, preferred_element_type=jnp.float32)
    spectra_low = spectra.astype(jnp.bfloat16)

    row_hits = (crossing_row[0][:, None] == jnp.arange(length, dtype=jnp.int32)[None, :]).astype(
        jnp.bfloat16
    )
    slice_rows = jnp.dot(row_hits, spectra_low, preferred_element_type=jnp.float32).astype(jnp.bfloat16)
    extra = 128
    meta_grid = jnp.arange(extra, dtype=jnp.int32)[None, :]
    weight_place = jnp.asarray(np.eye(planes, extra), jnp.bfloat16)
    meta = jnp.dot(interp_weight[0], weight_place, preferred_element_type=jnp.float32)
    meta = meta + jnp.where(meta_grid == planes, crossing_line[0][:, None].astype(jnp.float32), 0.0)
    payload = jnp.concatenate([slice_rows, meta.astype(jnp.bfloat16)], axis=1)

    destination = crossing_dest[0, :, 0]
    onehot = (destination[:, None] == jnp.arange(devices_all, dtype=jnp.int32)[None, :]).astype(jnp.int32)
    earlier = jnp.cumsum(onehot, axis=0) - onehot
    slot_within = jnp.sum(earlier * onehot, axis=1)
    position = destination * capacity + slot_within
    placing = (jnp.arange(slot_count, dtype=jnp.int32)[:, None] == position[None, :]).astype(jnp.bfloat16)
    send = jnp.dot(placing, payload, preferred_element_type=jnp.float32).astype(jnp.bfloat16)
    width = 2 * length + extra
    got = lax.all_to_all(
        send.reshape(devices_all, capacity, width), ("slab", "grp"), split_axis=0, concat_axis=0, tiled=True
    ).reshape(slot_count, width)

    step_planes = 4
    weight_in = (
        got[:, 2 * length : 2 * length + planes].T.astype(jnp.float32).reshape(planes // step_planes, step_planes, slot_count)
    )
    line_in = got[:, 2 * length + planes].astype(jnp.int32).reshape(1, slot_count)

    inverse = np.concatenate(
        [
            np.concatenate([cosine_table, sine_table], axis=1),
            np.concatenate([-sine_table, cosine_table], axis=1),
        ],
        axis=0,
    )
    inverse_high, inverse_low = halves(
        inverse.reshape(2 * length, 2, slab_count, x_block).transpose(2, 1, 3, 0).reshape(2 * length, 2 * length)
    )
    along_x = pl.pallas_call(
        accumulate_and_transform,
        out_shape=jax.ShapeDtypeStruct((slab_count, 2, planes, x_block, lines_per), jnp.bfloat16),
        grid=(planes // step_planes,),
        in_specs=[
            pl.BlockSpec((1, step_planes, slot_count), lambda i: (i, 0, 0)),
            pl.BlockSpec((1, slot_count), lambda i: (0, 0)),
            pl.BlockSpec((slot_count, 2 * length), lambda i: (0, 0)),
            pl.BlockSpec((2 * length, 2 * length), lambda i: (0, 0)),
            pl.BlockSpec((2 * length, 2 * length), lambda i: (0, 0)),
        ],
        out_specs=pl.BlockSpec((slab_count, 2, step_planes, x_block, lines_per), lambda i: (0, 0, i, 0, 0)),
    )(weight_in, line_in, got, inverse_high, inverse_low)
    pencil = lax.all_to_all(along_x, "slab", split_axis=0, concat_axis=0, tiled=True)

    lhs = pencil.transpose(3, 4, 0, 1, 2).reshape(x_block * lines_per, 2 * length)
    z_table = inverse.reshape(2, slab_count, planes, 2 * length).transpose(1, 0, 2, 3).reshape(2 * length, 2 * length)
    z_high, z_low = halves(z_table)
    parts = []
    for part in range(2):
        columns = slice(part * length, (part + 1) * length)
        flat = jnp.dot(lhs, z_high[:, columns], preferred_element_type=jnp.float32)
        flat = flat + jnp.dot(lhs, z_low[:, columns], preferred_element_type=jnp.float32)
        parts.append(flat.reshape(x_block, lines_per, length))
    result = jnp.stack(parts)
    return result


def solution(mesh):
    return jax.shard_map(
        local,
        mesh=mesh,
        in_specs=(
            P(("slab", "grp"), None, None),
            P(("slab", "grp"), None),
            P(("slab", "grp"), None, None),
            P(("slab", "grp"), None),
            P(("slab", "grp"), None, None),
        ),
        out_specs=P(None, "slab", "grp", None),
        check_vma=False,
    )
```

```python
import math

import jax
import jax.numpy as jnp
import ml_dtypes
import numpy as np
from jax import lax
from jax.experimental import pallas as pl
from jax.sharding import PartitionSpec as P


def twiddles(length):
    index_grid = np.arange(length)
    phase_angle = (np.outer(index_grid, index_grid) % length) * (2.0 * np.pi / length)
    norm_scale = 1.0 / math.sqrt(length)
    return (np.cos(phase_angle) * norm_scale, np.sin(phase_angle) * norm_scale)


def halves(values):
    high = values.astype(ml_dtypes.bfloat16)
    low = (values - high.astype(np.float64)).astype(ml_dtypes.bfloat16)
    return jnp.asarray(high), jnp.asarray(low)


def accumulate_and_transform(weight_ref, line_ref, rows_ref, inverse_high_ref, inverse_low_ref, out_ref):
    weights = weight_ref[0]
    lines = out_ref.shape[-1]
    hit = line_ref[...] == lax.broadcasted_iota(jnp.int32, (lines, weights.shape[1]), 0)
    spread = jnp.concatenate(
        [jnp.where(hit, weights[plane : plane + 1, :], 0.0) for plane in range(weights.shape[0])], axis=0
    )
    volume = jnp.dot(spread.astype(jnp.bfloat16), rows_ref[...], preferred_element_type=jnp.float32)
    volume_high = volume.astype(jnp.bfloat16)
    volume_low = (volume - volume_high.astype(jnp.float32)).astype(jnp.bfloat16)
    contract = (((1,), (1,)), ((), ()))
    along = lax.dot_general(inverse_high_ref[...], volume_high, contract, preferred_element_type=jnp.float32)
    along = along + lax.dot_general(inverse_high_ref[...], volume_low, contract, preferred_element_type=jnp.float32)
    along = along + lax.dot_general(inverse_low_ref[...], volume_high, contract, preferred_element_type=jnp.float32)
    blocks, _, parts, x_in, lanes = out_ref.shape
    for part in range(parts):
        piece = along[:, part * lanes : (part + 1) * lanes].reshape(blocks, 2, x_in, lanes)
        out_ref[:, :, part, :, :] = piece.astype(out_ref.dtype)


def local(images, crossing_row, crossing_dest, crossing_line, interp_weight):
    high = lax.Precision.HIGH
    length = images.shape[1]
    crossings = crossing_row.shape[1]
    slab_count = lax.axis_size("slab")
    group_count = lax.axis_size("grp")
    devices_all = slab_count * group_count
    planes = length // slab_count
    lines_per = length // group_count
    capacity = 2 * crossings // devices_all
    slot_count = devices_all * capacity
    x_block = length // slab_count
    cosine_table, sine_table = twiddles(length)

    image = images[0]
    forward_y = jnp.asarray(np.concatenate([cosine_table, -sine_table], axis=0), jnp.float32)
    along_y = jnp.dot(forward_y, image, precision=high, preferred_element_type=jnp.float32)
    from_real = jnp.asarray(np.concatenate([cosine_table, -sine_table], axis=1), jnp.float32)
    from_imag = jnp.asarray(np.concatenate([sine_table, cosine_table], axis=1), jnp.float32)
    spectra = jnp.dot(along_y[:length], from_real, precision=high, preferred_element_type=jnp.float32)
    spectra = spectra + jnp.dot(along_y[length:], from_imag, precision=high, preferred_element_type=jnp.float32)
    spectra_low = spectra.astype(jnp.bfloat16)

    row_hits = (crossing_row[0][:, None] == jnp.arange(length, dtype=jnp.int32)[None, :]).astype(
        jnp.bfloat16
    )
    slice_rows = jnp.dot(row_hits, spectra_low, preferred_element_type=jnp.float32).astype(jnp.bfloat16)
    extra = 128
    meta_grid = jnp.arange(extra, dtype=jnp.int32)[None, :]
    weight_place = jnp.asarray(np.eye(planes, extra), jnp.bfloat16)
    meta = jnp.dot(interp_weight[0], weight_place, preferred_element_type=jnp.float32)
    meta = meta + jnp.where(meta_grid == planes, crossing_line[0][:, None].astype(jnp.float32), 0.0)
    payload = jnp.concatenate([slice_rows, meta.astype(jnp.bfloat16)], axis=1)

    destination = crossing_dest[0, :, 0]
    onehot = (destination[:, None] == jnp.arange(devices_all, dtype=jnp.int32)[None, :]).astype(jnp.int32)
    earlier = jnp.cumsum(onehot, axis=0) - onehot
    slot_within = jnp.sum(earlier * onehot, axis=1)
    position = destination * capacity + slot_within
    placing = (jnp.arange(slot_count, dtype=jnp.int32)[:, None] == position[None, :]).astype(jnp.bfloat16)
    send = jnp.dot(placing, payload, preferred_element_type=jnp.float32).astype(jnp.bfloat16)
    width = 2 * length + extra
    got = lax.all_to_all(
        send.reshape(devices_all, capacity, width), ("slab", "grp"), split_axis=0, concat_axis=0, tiled=True
    ).reshape(slot_count, width)

    step_planes = 4
    weight_in = (
        got[:, 2 * length : 2 * length + planes].T.astype(jnp.float32).reshape(planes // step_planes, step_planes, slot_count)
    )
    line_in = got[:, 2 * length + planes].astype(jnp.int32).reshape(1, slot_count)

    inverse = np.concatenate(
        [
            np.concatenate([cosine_table, sine_table], axis=1),
            np.concatenate([-sine_table, cosine_table], axis=1),
        ],
        axis=0,
    )
    inverse_high, inverse_low = halves(
        inverse.reshape(2 * length, 2, slab_count, x_block).transpose(2, 1, 3, 0).reshape(2 * length, 2 * length)
    )
    along_x = pl.pallas_call(
        accumulate_and_transform,
        out_shape=jax.ShapeDtypeStruct((slab_count, 2, planes, x_block, lines_per), jnp.bfloat16),
        grid=(planes // step_planes,),
        in_specs=[
            pl.BlockSpec((1, step_planes, slot_count), lambda i: (i, 0, 0)),
            pl.BlockSpec((1, slot_count), lambda i: (0, 0)),
            pl.BlockSpec((slot_count, 2 * length), lambda i: (0, 0)),
            pl.BlockSpec((2 * length, 2 * length), lambda i: (0, 0)),
            pl.BlockSpec((2 * length, 2 * length), lambda i: (0, 0)),
        ],
        out_specs=pl.BlockSpec((slab_count, 2, step_planes, x_block, lines_per), lambda i: (0, 0, i, 0, 0)),
    )(weight_in, line_in, got, inverse_high, inverse_low)
    slab_index = lax.axis_index("slab")
    pencil = jnp.zeros_like(along_x)
    for shift in range(slab_count):
        piece = lax.dynamic_index_in_dim(along_x, (slab_index + shift) % slab_count, axis=0, keepdims=True)
        if shift:
            pairs = [(source, (source + shift) % slab_count) for source in range(slab_count)]
            piece = lax.ppermute(piece, "slab", pairs)
        pencil = lax.dynamic_update_index_in_dim(pencil, piece, (slab_index - shift) % slab_count, axis=0)

    lhs = pencil.transpose(3, 4, 0, 1, 2).reshape(x_block * lines_per, 2 * length)
    z_table = inverse.reshape(2, slab_count, planes, 2 * length).transpose(1, 0, 2, 3).reshape(2 * length, 2 * length)
    z_high, z_low = halves(z_table)
    parts = []
    for part in range(2):
        columns = slice(part * length, (part + 1) * length)
        flat = jnp.dot(lhs, z_high[:, columns], preferred_element_type=jnp.float32)
        flat = flat + jnp.dot(lhs, z_low[:, columns], preferred_element_type=jnp.float32)
        parts.append(flat.reshape(x_block, lines_per, length))
    result = jnp.stack(parts)
    return result


def solution(mesh):
    return jax.shard_map(
        local,
        mesh=mesh,
        in_specs=(
            P(("slab", "grp"), None, None),
            P(("slab", "grp"), None),
            P(("slab", "grp"), None, None),
            P(("slab", "grp"), None),
            P(("slab", "grp"), None, None),
        ),
        out_specs=P(None, "slab", "grp", None),
        check_vma=False,
    )
```

```python
import math

import jax
import jax.numpy as jnp
import ml_dtypes
import numpy as np
from jax import lax
from jax.experimental import pallas as pl
from jax.sharding import PartitionSpec as P


def twiddles(length):
    index_grid = np.arange(length)
    phase_angle = (np.outer(index_grid, index_grid) % length) * (2.0 * np.pi / length)
    norm_scale = 1.0 / math.sqrt(length)
    return (np.cos(phase_angle) * norm_scale, np.sin(phase_angle) * norm_scale)


def halves(values):
    high = values.astype(ml_dtypes.bfloat16)
    low = (values - high.astype(np.float64)).astype(ml_dtypes.bfloat16)
    return jnp.asarray(high), jnp.asarray(low)


def accumulate_and_transform(weight_ref, line_ref, rows_ref, inverse_high_ref, inverse_low_ref, out_ref):
    weights = weight_ref[0]
    lines = out_ref.shape[-1]
    hit = line_ref[...] == lax.broadcasted_iota(jnp.int32, (lines, weights.shape[1]), 0)
    spread = jnp.concatenate(
        [jnp.where(hit, weights[plane : plane + 1, :], 0.0) for plane in range(weights.shape[0])], axis=0
    )
    volume = jnp.dot(spread.astype(jnp.bfloat16), rows_ref[...], preferred_element_type=jnp.float32)
    volume_high = volume.astype(jnp.bfloat16)
    volume_low = (volume - volume_high.astype(jnp.float32)).astype(jnp.bfloat16)
    contract = (((1,), (1,)), ((), ()))
    along = lax.dot_general(inverse_high_ref[...], volume_high, contract, preferred_element_type=jnp.float32)
    along = along + lax.dot_general(inverse_high_ref[...], volume_low, contract, preferred_element_type=jnp.float32)
    along = along + lax.dot_general(inverse_low_ref[...], volume_high, contract, preferred_element_type=jnp.float32)
    blocks, _, parts, x_in, lanes = out_ref.shape
    for part in range(parts):
        piece = along[:, part * lanes : (part + 1) * lanes].reshape(blocks, 2, x_in, lanes)
        out_ref[:, :, part, :, :] = piece.astype(out_ref.dtype)


def local(images, crossing_row, crossing_dest, crossing_line, interp_weight):
    high = lax.Precision.HIGH
    length = images.shape[1]
    crossings = crossing_row.shape[1]
    slab_count = lax.axis_size("slab")
    group_count = lax.axis_size("grp")
    devices_all = slab_count * group_count
    planes = length // slab_count
    lines_per = length // group_count
    capacity = 2 * crossings // devices_all
    slot_count = devices_all * capacity
    x_block = length // slab_count
    cosine_table, sine_table = twiddles(length)

    image = images[0]
    forward_y = jnp.asarray(np.concatenate([cosine_table, -sine_table], axis=0), jnp.float32)
    along_y = jnp.dot(forward_y, image, precision=high, preferred_element_type=jnp.float32)
    from_real = jnp.asarray(np.concatenate([cosine_table, -sine_table], axis=1), jnp.float32)
    from_imag = jnp.asarray(np.concatenate([sine_table, cosine_table], axis=1), jnp.float32)
    spectra = jnp.dot(along_y[:length], from_real, precision=high, preferred_element_type=jnp.float32)
    spectra = spectra + jnp.dot(along_y[length:], from_imag, precision=high, preferred_element_type=jnp.float32)
    spectra_low = spectra.astype(jnp.bfloat16)

    row_hits = (crossing_row[0][:, None] == jnp.arange(length, dtype=jnp.int32)[None, :]).astype(
        jnp.bfloat16
    )
    slice_rows = jnp.dot(row_hits, spectra_low, preferred_element_type=jnp.float32).astype(jnp.bfloat16)
    extra = 128
    meta_grid = jnp.arange(extra, dtype=jnp.int32)[None, :]
    weight_place = jnp.asarray(np.eye(planes, extra), jnp.bfloat16)
    meta = jnp.dot(interp_weight[0], weight_place, preferred_element_type=jnp.float32)
    meta = meta + jnp.where(meta_grid == planes, crossing_line[0][:, None].astype(jnp.float32), 0.0)
    payload = jnp.concatenate([slice_rows, meta.astype(jnp.bfloat16)], axis=1)

    destination = crossing_dest[0, :, 0]
    onehot = (destination[:, None] == jnp.arange(devices_all, dtype=jnp.int32)[None, :]).astype(jnp.int32)
    earlier = jnp.cumsum(onehot, axis=0) - onehot
    slot_within = jnp.sum(earlier * onehot, axis=1)
    position = destination * capacity + slot_within
    placing = (jnp.arange(slot_count, dtype=jnp.int32)[:, None] == position[None, :]).astype(jnp.bfloat16)
    send = jnp.dot(placing, payload, preferred_element_type=jnp.float32).astype(jnp.bfloat16)
    width = 2 * length + extra
    got = lax.all_to_all(
        send.reshape(devices_all, capacity, width), ("slab", "grp"), split_axis=0, concat_axis=0, tiled=True
    ).reshape(slot_count, width)

    step_planes = 8
    weight_in = (
        got[:, 2 * length : 2 * length + planes].T.astype(jnp.float32).reshape(planes // step_planes, step_planes, slot_count)
    )
    line_in = got[:, 2 * length + planes].astype(jnp.int32).reshape(1, slot_count)

    inverse = np.concatenate(
        [
            np.concatenate([cosine_table, sine_table], axis=1),
            np.concatenate([-sine_table, cosine_table], axis=1),
        ],
        axis=0,
    )
    inverse_high, inverse_low = halves(
        inverse.reshape(2 * length, 2, slab_count, x_block).transpose(2, 1, 3, 0).reshape(2 * length, 2 * length)
    )
    along_x = pl.pallas_call(
        accumulate_and_transform,
        out_shape=jax.ShapeDtypeStruct((slab_count, 2, planes, x_block, lines_per), jnp.bfloat16),
        grid=(planes // step_planes,),
        in_specs=[
            pl.BlockSpec((1, step_planes, slot_count), lambda i: (i, 0, 0)),
            pl.BlockSpec((1, slot_count), lambda i: (0, 0)),
            pl.BlockSpec((slot_count, 2 * length), lambda i: (0, 0)),
            pl.BlockSpec((2 * length, 2 * length), lambda i: (0, 0)),
            pl.BlockSpec((2 * length, 2 * length), lambda i: (0, 0)),
        ],
        out_specs=pl.BlockSpec((slab_count, 2, step_planes, x_block, lines_per), lambda i: (0, 0, i, 0, 0)),
    )(weight_in, line_in, got, inverse_high, inverse_low)
    pencil = lax.all_to_all(along_x, "slab", split_axis=0, concat_axis=0, tiled=True)

    lhs = pencil.transpose(3, 4, 0, 1, 2).reshape(x_block * lines_per, 2 * length)
    z_table = inverse.reshape(2, slab_count, planes, 2 * length).transpose(1, 0, 2, 3).reshape(2 * length, 2 * length)
    z_high, z_low = halves(z_table)
    parts = []
    for part in range(2):
        columns = slice(part * length, (part + 1) * length)
        flat = jnp.dot(lhs, z_high[:, columns], preferred_element_type=jnp.float32)
        flat = flat + jnp.dot(lhs, z_low[:, columns], preferred_element_type=jnp.float32)
        parts.append(flat.reshape(x_block, lines_per, length))
    result = jnp.stack(parts)
    return result


def solution(mesh):
    return jax.shard_map(
        local,
        mesh=mesh,
        in_specs=(
            P(("slab", "grp"), None, None),
            P(("slab", "grp"), None),
            P(("slab", "grp"), None, None),
            P(("slab", "grp"), None),
            P(("slab", "grp"), None, None),
        ),
        out_specs=P(None, "slab", "grp", None),
        check_vma=False,
    )
```

```python
import math

import jax
import jax.numpy as jnp
import ml_dtypes
import numpy as np
from jax import lax
from jax.experimental import pallas as pl
from jax.sharding import PartitionSpec as P


def twiddles(length):
    index_grid = np.arange(length)
    phase_angle = (np.outer(index_grid, index_grid) % length) * (2.0 * np.pi / length)
    norm_scale = 1.0 / math.sqrt(length)
    return (np.cos(phase_angle) * norm_scale, np.sin(phase_angle) * norm_scale)


def halves(values):
    high = values.astype(ml_dtypes.bfloat16)
    low = (values - high.astype(np.float64)).astype(ml_dtypes.bfloat16)
    return jnp.asarray(high), jnp.asarray(low)


def accumulate_and_transform(weight_ref, line_ref, rows_ref, inverse_high_ref, inverse_low_ref, out_ref):
    weights = weight_ref[0]
    lines = out_ref.shape[-1]
    hit = line_ref[...] == lax.broadcasted_iota(jnp.int32, (lines, weights.shape[1]), 0)
    spread = jnp.concatenate(
        [jnp.where(hit, weights[plane : plane + 1, :], 0.0) for plane in range(weights.shape[0])], axis=0
    )
    volume = jnp.dot(spread.astype(jnp.bfloat16), rows_ref[...], preferred_element_type=jnp.float32)
    volume_high = volume.astype(jnp.bfloat16)
    volume_low = (volume - volume_high.astype(jnp.float32)).astype(jnp.bfloat16)
    contract = (((1,), (1,)), ((), ()))
    along = lax.dot_general(inverse_high_ref[...], volume_high, contract, preferred_element_type=jnp.float32)
    along = along + lax.dot_general(inverse_high_ref[...], volume_low, contract, preferred_element_type=jnp.float32)
    along = along + lax.dot_general(inverse_low_ref[...], volume_high, contract, preferred_element_type=jnp.float32)
    blocks, _, parts, x_in, lanes = out_ref.shape
    for part in range(parts):
        piece = along[:, part * lanes : (part + 1) * lanes].reshape(blocks, 2, x_in, lanes)
        out_ref[:, :, part, :, :] = piece.astype(out_ref.dtype)


def local(images, crossing_row, crossing_dest, crossing_line, interp_weight):
    high = lax.Precision.HIGH
    length = images.shape[1]
    crossings = crossing_row.shape[1]
    slab_count = lax.axis_size("slab")
    group_count = lax.axis_size("grp")
    devices_all = slab_count * group_count
    planes = length // slab_count
    lines_per = length // group_count
    capacity = 2 * crossings // devices_all
    slot_count = devices_all * capacity
    x_block = length // slab_count
    cosine_table, sine_table = twiddles(length)

    image = images[0]
    forward_y = jnp.asarray(np.concatenate([cosine_table, -sine_table], axis=0), jnp.float32)
    along_y = jnp.dot(forward_y, image, precision=high, preferred_element_type=jnp.float32)
    from_real = jnp.asarray(np.concatenate([cosine_table, -sine_table], axis=1), jnp.float32)
    from_imag = jnp.asarray(np.concatenate([sine_table, cosine_table], axis=1), jnp.float32)
    spectra = jnp.dot(along_y[:length], from_real, precision=high, preferred_element_type=jnp.float32)
    spectra = spectra + jnp.dot(along_y[length:], from_imag, precision=high, preferred_element_type=jnp.float32)
    spectra_low = spectra.astype(jnp.bfloat16)

    row_hits = (crossing_row[0][:, None] == jnp.arange(length, dtype=jnp.int32)[None, :]).astype(
        jnp.bfloat16
    )
    slice_rows = jnp.dot(row_hits, spectra_low, preferred_element_type=jnp.float32).astype(jnp.bfloat16)
    extra = 128
    meta_grid = jnp.arange(extra, dtype=jnp.int32)[None, :]
    weight_place = jnp.asarray(np.eye(planes, extra), jnp.bfloat16)
    meta = jnp.dot(interp_weight[0], weight_place, preferred_element_type=jnp.float32)
    meta = meta + jnp.where(meta_grid == planes, crossing_line[0][:, None].astype(jnp.float32), 0.0)
    payload = jnp.concatenate([slice_rows, meta.astype(jnp.bfloat16)], axis=1)

    destination = crossing_dest[0, :, 0]
    onehot = (destination[:, None] == jnp.arange(devices_all, dtype=jnp.int32)[None, :]).astype(jnp.int32)
    earlier = jnp.cumsum(onehot, axis=0) - onehot
    slot_within = jnp.sum(earlier * onehot, axis=1)
    position = destination * capacity + slot_within
    placing = (jnp.arange(slot_count, dtype=jnp.int32)[:, None] == position[None, :]).astype(jnp.bfloat16)
    send = jnp.dot(placing, payload, preferred_element_type=jnp.float32).astype(jnp.bfloat16)
    width = 2 * length + extra
    got = lax.all_to_all(
        send.reshape(devices_all, capacity, width), ("slab", "grp"), split_axis=0, concat_axis=0, tiled=True
    ).reshape(slot_count, width)

    step_planes = 16
    weight_in = (
        got[:, 2 * length : 2 * length + planes].T.astype(jnp.float32).reshape(planes // step_planes, step_planes, slot_count)
    )
    line_in = got[:, 2 * length + planes].astype(jnp.int32).reshape(1, slot_count)

    inverse = np.concatenate(
        [
            np.concatenate([cosine_table, sine_table], axis=1),
            np.concatenate([-sine_table, cosine_table], axis=1),
        ],
        axis=0,
    )
    inverse_high, inverse_low = halves(
        inverse.reshape(2 * length, 2, slab_count, x_block).transpose(2, 1, 3, 0).reshape(2 * length, 2 * length)
    )
    along_x = pl.pallas_call(
        accumulate_and_transform,
        out_shape=jax.ShapeDtypeStruct((slab_count, 2, planes, x_block, lines_per), jnp.bfloat16),
        grid=(planes // step_planes,),
        in_specs=[
            pl.BlockSpec((1, step_planes, slot_count), lambda i: (i, 0, 0)),
            pl.BlockSpec((1, slot_count), lambda i: (0, 0)),
            pl.BlockSpec((slot_count, 2 * length), lambda i: (0, 0)),
            pl.BlockSpec((2 * length, 2 * length), lambda i: (0, 0)),
            pl.BlockSpec((2 * length, 2 * length), lambda i: (0, 0)),
        ],
        out_specs=pl.BlockSpec((slab_count, 2, step_planes, x_block, lines_per), lambda i: (0, 0, i, 0, 0)),
    )(weight_in, line_in, got, inverse_high, inverse_low)
    pencil = lax.all_to_all(along_x, "slab", split_axis=0, concat_axis=0, tiled=True)

    lhs = pencil.transpose(3, 4, 0, 1, 2).reshape(x_block * lines_per, 2 * length)
    z_table = inverse.reshape(2, slab_count, planes, 2 * length).transpose(1, 0, 2, 3).reshape(2 * length, 2 * length)
    z_high, z_low = halves(z_table)
    parts = []
    for part in range(2):
        columns = slice(part * length, (part + 1) * length)
        flat = jnp.dot(lhs, z_high[:, columns], preferred_element_type=jnp.float32)
        flat = flat + jnp.dot(lhs, z_low[:, columns], preferred_element_type=jnp.float32)
        parts.append(flat.reshape(x_block, lines_per, length))
    result = jnp.stack(parts)
    return result


def solution(mesh):
    return jax.shard_map(
        local,
        mesh=mesh,
        in_specs=(
            P(("slab", "grp"), None, None),
            P(("slab", "grp"), None),
            P(("slab", "grp"), None, None),
            P(("slab", "grp"), None),
            P(("slab", "grp"), None, None),
        ),
        out_specs=P(None, "slab", "grp", None),
        check_vma=False,
    )
```

```python
import math

import jax
import jax.numpy as jnp
import ml_dtypes
import numpy as np
from jax import lax
from jax.experimental import pallas as pl
from jax.sharding import PartitionSpec as P


def twiddles(length):
    index_grid = np.arange(length)
    phase_angle = (np.outer(index_grid, index_grid) % length) * (2.0 * np.pi / length)
    norm_scale = 1.0 / math.sqrt(length)
    return (np.cos(phase_angle) * norm_scale, np.sin(phase_angle) * norm_scale)


def halves(values):
    high = values.astype(ml_dtypes.bfloat16)
    low = (values - high.astype(np.float64)).astype(ml_dtypes.bfloat16)
    return jnp.asarray(high), jnp.asarray(low)


def accumulate_and_transform(weight_ref, line_ref, rows_ref, inverse_high_ref, inverse_low_ref, out_ref):
    weights = weight_ref[0]
    lines = out_ref.shape[-1]
    hit = line_ref[...] == lax.broadcasted_iota(jnp.int32, (lines, weights.shape[1]), 0)
    spread = jnp.concatenate(
        [jnp.where(hit, weights[plane : plane + 1, :], jnp.zeros((), weights.dtype)) for plane in range(weights.shape[0])],
        axis=0,
    )
    volume = jnp.dot(spread.astype(jnp.bfloat16), rows_ref[...], preferred_element_type=jnp.float32)
    volume_high = volume.astype(jnp.bfloat16)
    volume_low = (volume - volume_high.astype(jnp.float32)).astype(jnp.bfloat16)
    contract = (((1,), (1,)), ((), ()))
    along = lax.dot_general(inverse_high_ref[...], volume_high, contract, preferred_element_type=jnp.float32)
    along = along + lax.dot_general(inverse_high_ref[...], volume_low, contract, preferred_element_type=jnp.float32)
    along = along + lax.dot_general(inverse_low_ref[...], volume_high, contract, preferred_element_type=jnp.float32)
    blocks, _, parts, x_in, lanes = out_ref.shape
    for part in range(parts):
        piece = along[:, part * lanes : (part + 1) * lanes].reshape(blocks, 2, x_in, lanes)
        out_ref[:, :, part, :, :] = piece.astype(out_ref.dtype)


def local(images, crossing_row, crossing_dest, crossing_line, interp_weight):
    high = lax.Precision.HIGH
    length = images.shape[1]
    crossings = crossing_row.shape[1]
    slab_count = lax.axis_size("slab")
    group_count = lax.axis_size("grp")
    devices_all = slab_count * group_count
    planes = length // slab_count
    lines_per = length // group_count
    capacity = 2 * crossings // devices_all
    slot_count = devices_all * capacity
    x_block = length // slab_count
    cosine_table, sine_table = twiddles(length)

    image = images[0]
    forward_y = jnp.asarray(np.concatenate([cosine_table, -sine_table], axis=0), jnp.float32)
    along_y = jnp.dot(forward_y, image, precision=high, preferred_element_type=jnp.float32)
    from_real = jnp.asarray(np.concatenate([cosine_table, -sine_table], axis=1), jnp.float32)
    from_imag = jnp.asarray(np.concatenate([sine_table, cosine_table], axis=1), jnp.float32)
    spectra = jnp.dot(along_y[:length], from_real, precision=high, preferred_element_type=jnp.float32)
    spectra = spectra + jnp.dot(along_y[length:], from_imag, precision=high, preferred_element_type=jnp.float32)
    spectra_low = spectra.astype(jnp.bfloat16)

    row_hits = (crossing_row[0][:, None] == jnp.arange(length, dtype=jnp.int32)[None, :]).astype(
        jnp.bfloat16
    )
    slice_rows = jnp.dot(row_hits, spectra_low, preferred_element_type=jnp.float32).astype(jnp.bfloat16)
    extra = 128
    meta_grid = jnp.arange(extra, dtype=jnp.int32)[None, :]
    weight_place = jnp.asarray(np.eye(planes, extra), jnp.bfloat16)
    meta = jnp.dot(interp_weight[0], weight_place, preferred_element_type=jnp.float32)
    meta = meta + jnp.where(meta_grid == planes, crossing_line[0][:, None].astype(jnp.float32), 0.0)
    payload = jnp.concatenate([slice_rows, meta.astype(jnp.bfloat16)], axis=1)

    destination = crossing_dest[0, :, 0]
    onehot = (destination[:, None] == jnp.arange(devices_all, dtype=jnp.int32)[None, :]).astype(jnp.int32)
    earlier = jnp.cumsum(onehot, axis=0) - onehot
    slot_within = jnp.sum(earlier * onehot, axis=1)
    position = destination * capacity + slot_within
    placing = (jnp.arange(slot_count, dtype=jnp.int32)[:, None] == position[None, :]).astype(jnp.bfloat16)
    send = jnp.dot(placing, payload, preferred_element_type=jnp.float32).astype(jnp.bfloat16)
    width = 2 * length + extra
    got = lax.all_to_all(
        send.reshape(devices_all, capacity, width), ("slab", "grp"), split_axis=0, concat_axis=0, tiled=True
    ).reshape(slot_count, width)

    step_planes = 8
    weight_in = (
        got[:, 2 * length : 2 * length + planes].T.reshape(planes // step_planes, step_planes, slot_count)
    )
    line_in = got[:, 2 * length + planes].astype(jnp.int32).reshape(1, slot_count)

    inverse = np.concatenate(
        [
            np.concatenate([cosine_table, sine_table], axis=1),
            np.concatenate([-sine_table, cosine_table], axis=1),
        ],
        axis=0,
    )
    inverse_high, inverse_low = halves(
        inverse.reshape(2 * length, 2, slab_count, x_block).transpose(2, 1, 3, 0).reshape(2 * length, 2 * length)
    )
    along_x = pl.pallas_call(
        accumulate_and_transform,
        out_shape=jax.ShapeDtypeStruct((slab_count, 2, planes, x_block, lines_per), jnp.bfloat16),
        grid=(planes // step_planes,),
        in_specs=[
            pl.BlockSpec((1, step_planes, slot_count), lambda i: (i, 0, 0)),
            pl.BlockSpec((1, slot_count), lambda i: (0, 0)),
            pl.BlockSpec((slot_count, 2 * length), lambda i: (0, 0)),
            pl.BlockSpec((2 * length, 2 * length), lambda i: (0, 0)),
            pl.BlockSpec((2 * length, 2 * length), lambda i: (0, 0)),
        ],
        out_specs=pl.BlockSpec((slab_count, 2, step_planes, x_block, lines_per), lambda i: (0, 0, i, 0, 0)),
    )(weight_in, line_in, got, inverse_high, inverse_low)
    pencil = lax.all_to_all(along_x, "slab", split_axis=0, concat_axis=0, tiled=True)

    lhs = pencil.transpose(3, 4, 0, 1, 2).reshape(x_block * lines_per, 2 * length)
    z_table = inverse.reshape(2, slab_count, planes, 2 * length).transpose(1, 0, 2, 3).reshape(2 * length, 2 * length)
    z_high, z_low = halves(z_table)
    parts = []
    for part in range(2):
        columns = slice(part * length, (part + 1) * length)
        flat = jnp.dot(lhs, z_high[:, columns], preferred_element_type=jnp.float32)
        flat = flat + jnp.dot(lhs, z_low[:, columns], preferred_element_type=jnp.float32)
        parts.append(flat.reshape(x_block, lines_per, length))
    result = jnp.stack(parts)
    return result


def solution(mesh):
    return jax.shard_map(
        local,
        mesh=mesh,
        in_specs=(
            P(("slab", "grp"), None, None),
            P(("slab", "grp"), None),
            P(("slab", "grp"), None, None),
            P(("slab", "grp"), None),
            P(("slab", "grp"), None, None),
        ),
        out_specs=P(None, "slab", "grp", None),
        check_vma=False,
    )
```

```python
import math

import jax
import jax.numpy as jnp
import ml_dtypes
import numpy as np
from jax import lax
from jax.experimental import pallas as pl
from jax.sharding import PartitionSpec as P


def twiddles(length):
    index_grid = np.arange(length)
    phase_angle = (np.outer(index_grid, index_grid) % length) * (2.0 * np.pi / length)
    norm_scale = 1.0 / math.sqrt(length)
    return (np.cos(phase_angle) * norm_scale, np.sin(phase_angle) * norm_scale)


def halves(values):
    high = values.astype(ml_dtypes.bfloat16)
    low = (values - high.astype(np.float64)).astype(ml_dtypes.bfloat16)
    return jnp.asarray(high), jnp.asarray(low)


def accumulate_and_transform(weight_ref, line_ref, rows_ref, inverse_high_ref, inverse_low_ref, out_ref):
    weights = weight_ref[0]
    lines = out_ref.shape[-1]
    hit = line_ref[...] == lax.broadcasted_iota(jnp.int32, (lines, weights.shape[1]), 0)
    spread = jnp.concatenate(
        [jnp.where(hit, weights[plane : plane + 1, :], jnp.zeros((), weights.dtype)) for plane in range(weights.shape[0])],
        axis=0,
    )
    volume = jnp.dot(spread.astype(jnp.bfloat16), rows_ref[...], preferred_element_type=jnp.float32)
    volume_high = volume.astype(jnp.bfloat16)
    volume_low = (volume - volume_high.astype(jnp.float32)).astype(jnp.bfloat16)
    contract = (((1,), (1,)), ((), ()))
    along = lax.dot_general(inverse_high_ref[...], volume_high, contract, preferred_element_type=jnp.float32)
    along = along + lax.dot_general(inverse_high_ref[...], volume_low, contract, preferred_element_type=jnp.float32)
    along = along + lax.dot_general(inverse_low_ref[...], volume_high, contract, preferred_element_type=jnp.float32)
    blocks, _, parts, x_in, lanes = out_ref.shape
    for part in range(parts):
        piece = along[:, part * lanes : (part + 1) * lanes].reshape(blocks, 2, x_in, lanes)
        out_ref[:, :, part, :, :] = piece.astype(out_ref.dtype)


def local(images, crossing_row, crossing_dest, crossing_line, interp_weight):
    high = lax.Precision.HIGH
    length = images.shape[1]
    crossings = crossing_row.shape[1]
    slab_count = lax.axis_size("slab")
    group_count = lax.axis_size("grp")
    devices_all = slab_count * group_count
    planes = length // slab_count
    lines_per = length // group_count
    capacity = 2 * crossings // devices_all
    slot_count = devices_all * capacity
    x_block = length // slab_count
    cosine_table, sine_table = twiddles(length)

    image = images[0]
    forward_y = jnp.asarray(np.concatenate([cosine_table, -sine_table], axis=0), jnp.float32)
    along_y = jnp.dot(forward_y, image, precision=high, preferred_element_type=jnp.float32)
    from_real = jnp.asarray(np.concatenate([cosine_table, -sine_table], axis=1), jnp.float32)
    from_imag = jnp.asarray(np.concatenate([sine_table, cosine_table], axis=1), jnp.float32)
    spectra = jnp.dot(along_y[:length], from_real, precision=high, preferred_element_type=jnp.float32)
    spectra = spectra + jnp.dot(along_y[length:], from_imag, precision=high, preferred_element_type=jnp.float32)
    spectra_low = spectra.astype(jnp.bfloat16)

    row_hits = (crossing_row[0][:, None] == jnp.arange(length, dtype=jnp.int32)[None, :]).astype(
        jnp.bfloat16
    )
    slice_rows = jnp.dot(row_hits, spectra_low, preferred_element_type=jnp.float32).astype(jnp.bfloat16)
    extra = 128
    meta_grid = jnp.arange(extra, dtype=jnp.int32)[None, :]
    weight_place = jnp.asarray(np.eye(planes, extra), jnp.bfloat16)
    meta = jnp.dot(interp_weight[0], weight_place, preferred_element_type=jnp.float32)
    meta = meta + jnp.where(meta_grid == planes, crossing_line[0][:, None].astype(jnp.float32), 0.0)
    payload = jnp.concatenate([slice_rows, meta.astype(jnp.bfloat16)], axis=1)

    destination = crossing_dest[0, :, 0]
    onehot = (destination[:, None] == jnp.arange(devices_all, dtype=jnp.int32)[None, :]).astype(jnp.int32)
    earlier = jnp.cumsum(onehot, axis=0) - onehot
    slot_within = jnp.sum(earlier * onehot, axis=1)
    position = destination * capacity + slot_within
    placing = (jnp.arange(slot_count, dtype=jnp.int32)[:, None] == position[None, :]).astype(jnp.bfloat16)
    send = jnp.dot(placing, payload, preferred_element_type=jnp.float32).astype(jnp.bfloat16)
    width = 2 * length + extra
    got = lax.all_to_all(
        send.reshape(devices_all, capacity, width), ("slab", "grp"), split_axis=0, concat_axis=0, tiled=True
    ).reshape(slot_count, width)

    step_planes = 8
    weight_in = (
        got[:, 2 * length : 2 * length + planes].T.reshape(planes // step_planes, step_planes, slot_count)
    )
    line_in = got[:, 2 * length + planes].astype(jnp.int32).reshape(1, slot_count)

    inverse = np.concatenate(
        [
            np.concatenate([cosine_table, sine_table], axis=1),
            np.concatenate([-sine_table, cosine_table], axis=1),
        ],
        axis=0,
    )
    inverse_high, inverse_low = halves(
        inverse.reshape(2 * length, 2, slab_count, x_block).transpose(2, 1, 3, 0).reshape(2 * length, 2 * length)
    )
    along_x = pl.pallas_call(
        accumulate_and_transform,
        out_shape=jax.ShapeDtypeStruct((slab_count, 2, planes, x_block, lines_per), jnp.bfloat16),
        grid=(planes // step_planes,),
        in_specs=[
            pl.BlockSpec((1, step_planes, slot_count), lambda i: (i, 0, 0)),
            pl.BlockSpec((1, slot_count), lambda i: (0, 0)),
            pl.BlockSpec((slot_count, 2 * length), lambda i: (0, 0)),
            pl.BlockSpec((2 * length, 2 * length), lambda i: (0, 0)),
            pl.BlockSpec((2 * length, 2 * length), lambda i: (0, 0)),
        ],
        out_specs=pl.BlockSpec((slab_count, 2, step_planes, x_block, lines_per), lambda i: (0, 0, i, 0, 0)),
    )(weight_in, line_in, got, inverse_high, inverse_low)
    pencil = lax.all_to_all(along_x, "slab", split_axis=0, concat_axis=0, tiled=True)

    lhs = pencil.transpose(3, 4, 0, 1, 2).reshape(x_block * lines_per, 2 * length)
    z_table = inverse.reshape(2, slab_count, planes, 2 * length).transpose(1, 0, 2, 3).reshape(2 * length, 2 * length)
    z_high, z_low = halves(z_table)
    flat = jnp.dot(lhs, z_high, preferred_element_type=jnp.float32)
    flat = flat + jnp.dot(lhs, z_low, preferred_element_type=jnp.float32)
    parts = [flat[:, part * length : (part + 1) * length].reshape(x_block, lines_per, length) for part in range(2)]
    result = jnp.stack(parts)
    return result


def solution(mesh):
    return jax.shard_map(
        local,
        mesh=mesh,
        in_specs=(
            P(("slab", "grp"), None, None),
            P(("slab", "grp"), None),
            P(("slab", "grp"), None, None),
            P(("slab", "grp"), None),
            P(("slab", "grp"), None, None),
        ),
        out_specs=P(None, "slab", "grp", None),
        check_vma=False,
    )
```

```python
import math

import jax
import jax.numpy as jnp
import ml_dtypes
import numpy as np
from jax import lax
from jax.experimental import pallas as pl
from jax.sharding import PartitionSpec as P


def twiddles(length):
    index_grid = np.arange(length)
    phase_angle = (np.outer(index_grid, index_grid) % length) * (2.0 * np.pi / length)
    norm_scale = 1.0 / math.sqrt(length)
    return (np.cos(phase_angle) * norm_scale, np.sin(phase_angle) * norm_scale)


def halves(values):
    high = values.astype(ml_dtypes.bfloat16)
    low = (values - high.astype(np.float64)).astype(ml_dtypes.bfloat16)
    return jnp.asarray(high), jnp.asarray(low)


def accumulate_and_transform(weight_ref, line_ref, rows_ref, inverse_ref, out_ref):
    weights = weight_ref[0]
    lines = out_ref.shape[-1]
    hit = line_ref[...] == lax.broadcasted_iota(jnp.int32, (lines, weights.shape[1]), 0)
    spread = jnp.concatenate(
        [jnp.where(hit, weights[plane : plane + 1, :], jnp.zeros((), weights.dtype)) for plane in range(weights.shape[0])],
        axis=0,
    )
    volume = jnp.dot(spread.astype(jnp.bfloat16), rows_ref[...], preferred_element_type=jnp.float32)
    volume_high = volume.astype(jnp.bfloat16)
    volume_low = (volume - volume_high.astype(jnp.float32)).astype(jnp.bfloat16)
    stacked = jnp.concatenate([volume_high, volume_low, volume_high], axis=1)
    along = lax.dot_general(inverse_ref[...], stacked, (((1,), (1,)), ((), ())), preferred_element_type=jnp.float32)
    blocks, _, parts, x_in, lanes = out_ref.shape
    for part in range(parts):
        piece = along[:, part * lanes : (part + 1) * lanes].reshape(blocks, 2, x_in, lanes)
        out_ref[:, :, part, :, :] = piece.astype(out_ref.dtype)


def local(images, crossing_row, crossing_dest, crossing_line, interp_weight):
    high = lax.Precision.HIGH
    length = images.shape[1]
    crossings = crossing_row.shape[1]
    slab_count = lax.axis_size("slab")
    group_count = lax.axis_size("grp")
    devices_all = slab_count * group_count
    planes = length // slab_count
    lines_per = length // group_count
    capacity = 2 * crossings // devices_all
    slot_count = devices_all * capacity
    x_block = length // slab_count
    cosine_table, sine_table = twiddles(length)

    image = images[0]
    forward_y = jnp.asarray(np.concatenate([cosine_table, -sine_table], axis=0), jnp.float32)
    along_y = jnp.dot(forward_y, image, precision=high, preferred_element_type=jnp.float32)
    from_real = jnp.asarray(np.concatenate([cosine_table, -sine_table], axis=1), jnp.float32)
    from_imag = jnp.asarray(np.concatenate([sine_table, cosine_table], axis=1), jnp.float32)
    spectra = jnp.dot(along_y[:length], from_real, precision=high, preferred_element_type=jnp.float32)
    spectra = spectra + jnp.dot(along_y[length:], from_imag, precision=high, preferred_element_type=jnp.float32)
    spectra_low = spectra.astype(jnp.bfloat16)

    row_hits = (crossing_row[0][:, None] == jnp.arange(length, dtype=jnp.int32)[None, :]).astype(
        jnp.bfloat16
    )
    slice_rows = jnp.dot(row_hits, spectra_low, preferred_element_type=jnp.float32).astype(jnp.bfloat16)
    extra = 128
    meta_grid = jnp.arange(extra, dtype=jnp.int32)[None, :]
    weight_place = jnp.asarray(np.eye(planes, extra), jnp.bfloat16)
    meta = jnp.dot(interp_weight[0], weight_place, preferred_element_type=jnp.float32)
    meta = meta + jnp.where(meta_grid == planes, crossing_line[0][:, None].astype(jnp.float32), 0.0)
    payload = jnp.concatenate([slice_rows, meta.astype(jnp.bfloat16)], axis=1)

    destination = crossing_dest[0, :, 0]
    onehot = (destination[:, None] == jnp.arange(devices_all, dtype=jnp.int32)[None, :]).astype(jnp.int32)
    earlier = jnp.cumsum(onehot, axis=0) - onehot
    slot_within = jnp.sum(earlier * onehot, axis=1)
    position = destination * capacity + slot_within
    placing = (jnp.arange(slot_count, dtype=jnp.int32)[:, None] == position[None, :]).astype(jnp.bfloat16)
    send = jnp.dot(placing, payload, preferred_element_type=jnp.float32).astype(jnp.bfloat16)
    width = 2 * length + extra
    got = lax.all_to_all(
        send.reshape(devices_all, capacity, width), ("slab", "grp"), split_axis=0, concat_axis=0, tiled=True
    ).reshape(slot_count, width)

    step_planes = 8
    weight_in = (
        got[:, 2 * length : 2 * length + planes].T.reshape(planes // step_planes, step_planes, slot_count)
    )
    line_in = got[:, 2 * length + planes].astype(jnp.int32).reshape(1, slot_count)

    inverse = np.concatenate(
        [
            np.concatenate([cosine_table, sine_table], axis=1),
            np.concatenate([-sine_table, cosine_table], axis=1),
        ],
        axis=0,
    )
    inverse_high, inverse_low = halves(
        inverse.reshape(2 * length, 2, slab_count, x_block).transpose(2, 1, 3, 0).reshape(2 * length, 2 * length)
    )
    along_x = pl.pallas_call(
        accumulate_and_transform,
        out_shape=jax.ShapeDtypeStruct((slab_count, 2, planes, x_block, lines_per), jnp.bfloat16),
        grid=(planes // step_planes,),
        in_specs=[
            pl.BlockSpec((1, step_planes, slot_count), lambda i: (i, 0, 0)),
            pl.BlockSpec((1, slot_count), lambda i: (0, 0)),
            pl.BlockSpec((slot_count, 2 * length), lambda i: (0, 0)),
            pl.BlockSpec((2 * length, 6 * length), lambda i: (0, 0)),
        ],
        out_specs=pl.BlockSpec((slab_count, 2, step_planes, x_block, lines_per), lambda i: (0, 0, i, 0, 0)),
    )(weight_in, line_in, got, jnp.concatenate([inverse_high, inverse_high, inverse_low], axis=1))
    pencil = lax.all_to_all(along_x, "slab", split_axis=0, concat_axis=0, tiled=True)

    lhs = pencil.transpose(3, 4, 0, 1, 2).reshape(x_block * lines_per, 2 * length)
    z_table = inverse.reshape(2, slab_count, planes, 2 * length).transpose(1, 0, 2, 3).reshape(2 * length, 2 * length)
    z_high, z_low = halves(z_table)
    flat = jnp.dot(lhs, z_high, preferred_element_type=jnp.float32)
    flat = flat + jnp.dot(lhs, z_low, preferred_element_type=jnp.float32)
    parts = [flat[:, part * length : (part + 1) * length].reshape(x_block, lines_per, length) for part in range(2)]
    result = jnp.stack(parts)
    return result


def solution(mesh):
    return jax.shard_map(
        local,
        mesh=mesh,
        in_specs=(
            P(("slab", "grp"), None, None),
            P(("slab", "grp"), None),
            P(("slab", "grp"), None, None),
            P(("slab", "grp"), None),
            P(("slab", "grp"), None, None),
        ),
        out_specs=P(None, "slab", "grp", None),
        check_vma=False,
    )
```
